512 devices in a mesh: row: 64 (over x_lo, z, core), col: 8 (over y, x_hi).
Axes of the slice: x: 4 (x_hi: 2, x_lo: 2; x = x_hi * 2 + x_lo), y: 4, z: 16, core: 2. Of those that a mesh axis runs over, the one named last changes fastest.
Arguments:
- features: bfloat16 [128, 131072], P(None, 'row'), may hold values from -6 to 6
- weight_in: bfloat16 [128, 512], P(None, 'col'), may hold values from -0.5 to 0.5
- weight_out: bfloat16 [512, 64], replicated, may hold values from -0.25 to 0.25
- score_grad: bfloat16 [64, 131072], P('col', 'row'), may hold values from -0.011962891 to 0.011962891
- band_blocks: bfloat16 [1024, 3, 128, 128], P('row'), may hold values from -0.25 to 0.25
- long_blocks: bfloat16 [768, 128, 128], P('row'), may hold values from -0.25 to 0.25
- long_rows: int32 [64, 12], P('row'), may hold values from 0 to 15
- long_sources: int32 [64, 12], replicated, may hold values from 0 to 1023, as said below
- long_counts: int32 [64], replicated, may hold values from 1 to 12, as said below
Outputs:
- scores: bfloat16 [64, 131072], P('col', 'row')
- first_grad: float32 [128, 512], P(None, 'col')
- second_grad: float32 [512, 64], P('col')
The draws below stay inside these ranges and needn't reach their ends.
Inputs may be any that keep to these rules, and one draw needn't show every extreme that they name: `long_sources`: every slot's block column lies on a partition at cycle distance 1 to 3 from the slot's own partition (either direction, indices taken mod the number of partitions); over ALL 12 slots of a partition each of the 6 such partitions is read by exactly 2 slots. Slots s < long_counts[p] are live, the others are ignored; some partition has all 12 live.
All inputs are finite; a program needn't handle non-finite values.
Results may differ from the reference program's by a relative error of at most 0.0065.
Values may be sent and summed in bfloat16 or wider, within the bound.
No kernel may reach another device: no remote copies, remote signals or barrier semaphores. Data moves between devices by JAX's collectives and lax.ppermute only.
A program may use at most 64 MiB of HBM per device.

```python
import jax
import jax.numpy as jnp

BLK = 128
NB = 16
REACH = 3
CAP = 2
SLOTS = 12
F_IN = 128
H = 512
C = 64
BLOCKS = 1024
NODES = 131072
LONG_ALL = 768
N_ROW = 64


def draw_long_sources(key, part):
    key_order = jax.random.fold_in(key, 11)
    key_local = jax.random.fold_in(key, 12)
    offset_list = jnp.repeat(jnp.array([distance for distance in range(-REACH, REACH + 1) if distance != 0], jnp.int32), CAP)
    scores_int = jax.random.randint(key_order, (N_ROW, SLOTS), 0, 1 << 20) * SLOTS + jnp.arange(SLOTS, dtype=jnp.int32)[None, :]
    shuffle = jnp.argsort(scores_int, axis=1)
    offsets = offset_list[shuffle]
    partition = jnp.arange(N_ROW, dtype=jnp.int32)[:, None]
    owners = jnp.mod(partition + offsets, N_ROW)
    local_blocks = jax.random.randint(key_local, (N_ROW, SLOTS), 0, NB)
    return (owners * NB + local_blocks).astype(jnp.int32)


def draw_long_counts(key, part):
    first_draw = jax.random.randint(jax.random.fold_in(key, 21), (N_ROW,), 0, SLOTS + 1)
    second_draw = jax.random.randint(jax.random.fold_in(key, 22), (N_ROW,), 0, SLOTS + 1)
    counts_drawn = 1 + first_draw * second_draw // (SLOTS + 1)
    fullest = jax.random.randint(jax.random.fold_in(key, 23), (), 0, N_ROW)
    return jnp.where(jnp.arange(N_ROW, dtype=jnp.int32) == fullest, SLOTS, counts_drawn).astype(jnp.int32)


def plant(values, key, low, largest):
    longest = values.shape.index(max(values.shape))
    spots = []
    for shift in (0, 1):
        where = [jax.random.randint(jax.random.fold_in(key, axis), (), 0, length) for axis, length in enumerate(values.shape)]
        where[longest] = (where[longest] + shift) % values.shape[longest]
        spots.append(tuple(where))
    return values.at[spots[0]].set(low).at[spots[1]].set(largest)


def block_levels(stream_key, extent, pieces, least, largest):
    def one(dim, blocks):
        heights = jax.random.uniform(jax.random.fold_in(jax.random.fold_in(stream_key, 6), dim), (blocks,), jnp.float32, least / len(pieces), largest / len(pieces))
        return jnp.repeat(jnp.exp(heights), extent[dim] // blocks).reshape((-1,) + (1,) * (len(extent) - dim - 1))

    level = one(*pieces[0])
    for cut in pieces[1:]:
        level = level * one(*cut)
    return level


def noise(key, shape, width, bound, pieces=(), kind=jnp.bfloat16):
    drawn = jax.random.normal(key, shape, jnp.float32) * width
    if len(pieces) > 0:
        drawn = block_levels(key, shape, pieces, -0.22, 0.18) * drawn
    return jnp.clip(drawn, min=-bound, max=bound).astype(kind)


def setup_inputs(seed: int = 0) -> dict:
    seeds = jax.random.split(jax.random.key(seed), 10)
    features = noise(seeds[0], (F_IN, NODES), 1.0, 6.0, ((1, 64),))
    weight_in = noise(seeds[1], (F_IN, H), F_IN ** -0.5, 0.5, ((1, 8),))
    weight_out = noise(seeds[2], (H, C), H ** -0.5, 0.25)
    score_grad = noise(seeds[3], (C, NODES), 0.002, 0.011962891, ((0, 8), (1, 64)))
    band_blocks = noise(seeds[4], (BLOCKS, 3, BLK, BLK), (4 * BLK) ** -0.5, 0.25, ((0, 64),))
    long_blocks = noise(seeds[5], (LONG_ALL, BLK, BLK), (4 * BLK) ** -0.5, 0.25, ((0, 64),))
    long_rows = plant(jax.random.randint(seeds[6], (N_ROW, SLOTS), 0, NB), jax.random.fold_in(seeds[6], 1), 0, NB - 1).astype(jnp.int32)
    long_sources = draw_long_sources(jax.random.fold_in(seeds[9], 71), 0)
    long_counts = draw_long_counts(jax.random.fold_in(seeds[9], 71), 0)
    return {"features": features, "weight_in": weight_in, "weight_out": weight_out, "score_grad": score_grad, "band_blocks": band_blocks, "long_blocks": long_blocks, "long_rows": long_rows, "long_sources": long_sources, "long_counts": long_counts}


def slot_lists(long_rows, long_sources, long_counts):
    slot_order = jnp.arange(SLOTS, dtype=jnp.int32)
    is_live = (slot_order[None, :] < long_counts[:, None]).reshape(-1)
    targets = (jnp.arange(N_ROW, dtype=jnp.int32)[:, None] * NB + long_rows).reshape(-1).astype(jnp.int32)
    sources = long_sources.reshape(-1).astype(jnp.int32)
    return is_live, targets, sources


def band_product(values, band_blocks):
    rows_count = values.shape[0]
    blocks = values.reshape(rows_count, BLOCKS, BLK).astype(jnp.float32)
    band_wide = band_blocks.astype(jnp.float32)
    earlier = jnp.roll(blocks, 1, axis=1)
    onward = jnp.roll(blocks, -1, axis=1)
    summed = jnp.einsum('fgm,gnm->fgn', earlier, band_wide[:, 0])
    summed = summed + jnp.einsum('fgm,gnm->fgn', blocks, band_wide[:, 1])
    summed = summed + jnp.einsum('fgm,gnm->fgn', onward, band_wide[:, 2])
    return summed.reshape(rows_count, NODES)


def band_transpose(values, band_blocks):
    rows_count = values.shape[0]
    blocks = values.reshape(rows_count, BLOCKS, BLK).astype(jnp.float32)
    band_wide = band_blocks.astype(jnp.float32)
    to_prior = jnp.einsum('fgn,gnm->fgm', blocks, band_wide[:, 0])
    middle = jnp.einsum('fgn,gnm->fgm', blocks, band_wide[:, 1])
    to_later = jnp.einsum('fgn,gnm->fgm', blocks, band_wide[:, 2])
    summed = middle + jnp.roll(to_prior, -1, axis=1) + jnp.roll(to_later, 1, axis=1)
    return summed.reshape(rows_count, NODES)


def long_product(values, long_blocks, is_live, targets, sources):
    rows_count = values.shape[0]
    blocks = values.reshape(rows_count, BLOCKS, BLK).astype(jnp.float32)
    panels = jnp.take(blocks, sources, axis=1)
    contrib = jnp.einsum('fkm,knm->fkn', panels, long_blocks.astype(jnp.float32))
    contrib = contrib * is_live.astype(jnp.float32)[None, :, None]
    summed = jnp.zeros((rows_count, BLOCKS, BLK), jnp.float32).at[:, targets].add(contrib)
    return summed.reshape(rows_count, NODES)


def long_transpose(values, long_blocks, is_live, targets, sources):
    rows_count = values.shape[0]
    blocks = values.reshape(rows_count, BLOCKS, BLK).astype(jnp.float32)
    panels = jnp.take(blocks, targets, axis=1)
    contrib = jnp.einsum('fkn,knm->fkm', panels, long_blocks.astype(jnp.float32))
    contrib = contrib * is_live.astype(jnp.float32)[None, :, None]
    summed = jnp.zeros((rows_count, BLOCKS, BLK), jnp.float32).at[:, sources].add(contrib)
    return summed.reshape(rows_count, NODES)


def reference(features, weight_in, weight_out, score_grad, band_blocks, long_blocks, long_rows, long_sources, long_counts):
    is_live, targets, sources = slot_lists(long_rows, long_sources, long_counts)

    def aggregate(values):
        return band_product(values, band_blocks) + long_product(values, long_blocks, is_live, targets, sources)

    def aggregate_back(values):
        return band_transpose(values, band_blocks) + long_transpose(values, long_blocks, is_live, targets, sources)

    hidden_in = jnp.dot(weight_in.T, features, preferred_element_type=jnp.float32).astype(jnp.bfloat16)
    hidden_sum = aggregate(hidden_in)
    hidden_act = jax.nn.silu(hidden_sum).astype(jnp.bfloat16)
    class_in = jnp.dot(weight_out.T, hidden_act, preferred_element_type=jnp.float32).astype(jnp.bfloat16)
    scores = aggregate(class_in).astype(jnp.bfloat16)
    class_back = aggregate_back(score_grad).astype(jnp.bfloat16)
    second_grad = jnp.dot(hidden_act, class_back.T, preferred_element_type=jnp.float32)
    hidden_back = jnp.dot(weight_out, class_back, preferred_element_type=jnp.float32)
    sigmoid_val = jax.nn.sigmoid(hidden_sum)
    slope_back = (hidden_back * sigmoid_val * (1.0 + hidden_sum * (1.0 - sigmoid_val))).astype(jnp.bfloat16)
    input_back = aggregate_back(slope_back).astype(jnp.bfloat16)
    first_grad = jnp.dot(features, input_back.T, preferred_element_type=jnp.float32)
    return scores, first_grad, second_grad
```

```python
import jax
import jax.numpy as jnp
from jax import lax
from jax.sharding import PartitionSpec as P

BLK = 128
NB = 16
REACH = 3
SLOTS = 12
HI = lax.Precision.HIGHEST


def shifts():
    return [e for e in range(-REACH, REACH + 1) if e != 0]


def shift_index(e):
    return e + REACH if e < 0 else e + REACH - 1


def send_by(x, axis, by):
    devices = lax.axis_size(axis)
    return lax.ppermute(x, axis, [(i, (i + by) % devices) for i in range(devices)])


def swap_with(x, axis, mask):
    devices = lax.axis_size(axis)
    return lax.ppermute(x, axis, [(i, i ^ mask) for i in range(devices)])


def reading_blocks(long_sources, reader, owner):
    source = lax.dynamic_index_in_dim(long_sources, reader, 0, keepdims=False)
    hit = (source // NB) == owner
    rank = jnp.cumsum(hit.astype(jnp.int32)) - 1
    local = source % NB
    return [jnp.sum(jnp.where(hit & (rank == q), local, 0)) for q in range(2)]


def own_slot_pairs(long_sources, me, row_devices):
    source = lax.dynamic_index_in_dim(long_sources, me, 0, keepdims=False)
    owner = source // NB
    offset = jnp.mod(owner - me, row_devices)
    offset = jnp.where(offset > row_devices // 2, offset - row_devices, offset)
    same = (owner[:, None] == owner[None, :]) & (
        jnp.arange(SLOTS)[None, :] < jnp.arange(SLOTS)[:, None]
    )
    rank = jnp.sum(same.astype(jnp.int32), axis=1)
    position = jnp.where(offset < 0, offset + REACH, offset + REACH - 1)
    return offset, position * 2 + rank


def block(v, b):
    return lax.dynamic_slice_in_dim(v, b * BLK, BLK, axis=1)


def forward_sum(blocks, prev_edge, next_edge, panels, band_blocks, long_blocks, targets):
    earlier = jnp.concatenate([prev_edge[:, None], blocks[:, :-1]], 1)
    onward = jnp.concatenate([blocks[:, 1:], next_edge[:, None]], 1)
    near = jnp.einsum("fbm,bnm->fbn", earlier, band_blocks[:, 0], preferred_element_type=jnp.float32)
    near = near + jnp.einsum("fbm,bnm->fbn", blocks, band_blocks[:, 1], preferred_element_type=jnp.float32)
    near = near + jnp.einsum("fbm,bnm->fbn", onward, band_blocks[:, 2], preferred_element_type=jnp.float32)
    contrib = jnp.einsum("kfm,knm->kfn", panels, long_blocks, preferred_element_type=jnp.float32)
    far = jnp.einsum("kb,kfn->fbn", targets, contrib, precision=HI)
    return near + far


def local(
    features,
    weight_in,
    weight_out,
    score_grad,
    band_blocks,
    long_blocks,
    long_rows,
    long_sources,
    long_counts,
):
    row_devices = lax.axis_size("row")
    col_devices = lax.axis_size("col")
    me = lax.axis_index("row")
    col_index = lax.axis_index("col")
    row_ids = long_rows[0]
    hidden_count = weight_in.shape[1]
    class_count = score_grad.shape[0]
    nodes = features.shape[1]

    live_count = lax.dynamic_index_in_dim(long_counts, me, 0, keepdims=False)
    is_live = jnp.arange(SLOTS, dtype=jnp.int32) < live_count
    live = is_live.astype(jnp.float32)
    targets = (
        (row_ids[:, None] == jnp.arange(NB, dtype=jnp.int32)[None, :]) & is_live[:, None]
    ).astype(jnp.float32)
    offset, pair = own_slot_pairs(long_sources, me, row_devices)
    slot_of_pair = jnp.sum(
        jnp.where(pair[None, :] == jnp.arange(SLOTS)[:, None], jnp.arange(SLOTS)[None, :], 0), axis=1
    )

    hidden_in = jnp.einsum(
        "ih,in->hn", weight_in, features, preferred_element_type=jnp.float32
    ).astype(jnp.bfloat16)

    sg_blocks = score_grad.reshape(class_count, NB, BLK)
    sg_prior = jnp.einsum("fbn,bnm->fbm", sg_blocks, band_blocks[:, 0], preferred_element_type=jnp.float32)
    sg_middle = jnp.einsum("fbn,bnm->fbm", sg_blocks, band_blocks[:, 1], preferred_element_type=jnp.float32)
    sg_later = jnp.einsum("fbn,bnm->fbm", sg_blocks, band_blocks[:, 2], preferred_element_type=jnp.float32)
    sg_rows = jnp.take(sg_blocks, row_ids, axis=1)
    sg_contrib = jnp.einsum("fkn,knm->kfm", sg_rows, long_blocks, preferred_element_type=jnp.float32)
    sg_contrib = sg_contrib * live[:, None, None]
    sg_out = jnp.take(sg_contrib, slot_of_pair, axis=0)

    payloads = {}
    for e in shifts():
        reader = jnp.mod(me + e, row_devices)
        wanted = reading_blocks(long_sources, reader, me)
        parts = [block(hidden_in, b).astype(jnp.float32) for b in wanted]
        parts += [block(features, b).astype(jnp.float32) for b in wanted]
        t = shift_index(e) * 2
        parts += [sg_out[t], sg_out[t + 1]]
        if e == 1:
            parts += [
                hidden_in[:, nodes - BLK:].astype(jnp.float32),
                features[:, nodes - BLK:].astype(jnp.float32),
                sg_later[:, NB - 1],
            ]
        if e == -1:
            parts += [
                hidden_in[:, :BLK].astype(jnp.float32),
                features[:, :BLK].astype(jnp.float32),
                sg_prior[:, 0],
            ]
        payloads[e] = send_by(jnp.concatenate(parts, 0), "row", e)

    h_rows = hidden_count
    f_rows = features.shape[0]
    c_rows = class_count

    def unpack(x):
        i = 0
        out = []
        for size in (h_rows, h_rows, f_rows, f_rows, c_rows, c_rows, h_rows, f_rows, c_rows):
            if i >= x.shape[0]:
                break
            out.append(x[i:i + size])
            i += size
        return out

    arrived = {e: unpack(payloads[e]) for e in shifts()}
    hid_pool = jnp.stack([arrived[e][q] for e in shifts() for q in range(2)], 0)
    feat_pool = jnp.stack([arrived[e][2 + q] for e in shifts() for q in range(2)], 0)
    read_position = jnp.where(-offset < 0, -offset + REACH, -offset + REACH - 1)
    own_rank = pair % 2
    read_index = read_position * 2 + own_rank
    hid_panels = jnp.take(hid_pool, read_index, axis=0).astype(jnp.bfloat16)
    feat_panels = jnp.take(feat_pool, read_index, axis=0).astype(jnp.bfloat16)

    hid_blocks = hidden_in.reshape(h_rows, NB, BLK)
    hidden_sum = forward_sum(
        hid_blocks,
        arrived[1][6].astype(jnp.bfloat16),
        arrived[-1][6].astype(jnp.bfloat16),
        hid_panels,
        band_blocks,
        long_blocks,
        targets,
    ).reshape(h_rows, nodes)
    feat_blocks = features.reshape(f_rows, NB, BLK)
    feat_sum = forward_sum(
        feat_blocks,
        arrived[1][7].astype(jnp.bfloat16),
        arrived[-1][7].astype(jnp.bfloat16),
        feat_panels,
        band_blocks,
        long_blocks,
        targets,
    ).reshape(f_rows, nodes)

    zero_block = jnp.zeros((c_rows, 1, BLK), jnp.float32)
    sg_sum = (
        sg_middle
        + jnp.concatenate([sg_prior[:, 1:], zero_block], 1)
        + jnp.concatenate([zero_block, sg_later[:, :-1]], 1)
    )
    sg_in = jnp.stack([arrived[e][4 + q] for e in shifts() for q in range(2)], 0)
    land = []
    for e in shifts():
        sender = jnp.mod(me - e, row_devices)
        land += reading_blocks(long_sources, sender, me)
    land = jnp.stack(land)
    landing = (land[:, None] == jnp.arange(NB, dtype=jnp.int32)[None, :]).astype(jnp.float32)
    sg_sum = sg_sum + jnp.einsum("kb,kfm->fbm", landing, sg_in, precision=HI)
    sg_sum = sg_sum.at[:, 0].add(arrived[1][8])
    sg_sum = sg_sum.at[:, NB - 1].add(arrived[-1][8])
    class_back = sg_sum.reshape(c_rows, nodes).astype(jnp.bfloat16)

    hidden_act = jax.nn.silu(hidden_sum).astype(jnp.bfloat16)

    my_rows = lax.dynamic_slice_in_dim(weight_out, col_index * hidden_count, hidden_count, 0)
    class_part = jnp.einsum("hc,hn->cn", my_rows, hidden_act, preferred_element_type=jnp.float32)
    reduced = class_part.reshape(col_devices, c_rows, nodes)
    gathered = class_back.reshape(1, c_rows, nodes)
    mask = col_devices // 2
    while mask >= 1:
        bit = (col_index // mask) % 2
        halves = reduced.reshape(2, -1, c_rows, nodes)
        keep = lax.dynamic_index_in_dim(halves, bit, 0, keepdims=False)
        away = lax.dynamic_index_in_dim(halves, 1 - bit, 0, keepdims=False)
        count = away.shape[0]
        both = swap_with(jnp.concatenate([away, gathered.astype(jnp.float32)], 0), "col", mask)
        reduced = keep + both[:count]
        other = both[count:].astype(jnp.bfloat16)
        gathered = jnp.where(
            bit == 0,
            jnp.concatenate([gathered, other], 0),
            jnp.concatenate([other, gathered], 0),
        )
        mask //= 2
    class_in = reduced.reshape(c_rows, nodes).astype(jnp.bfloat16)
    order = []
    for j in range(col_devices):
        rev = 0
        bits = col_devices.bit_length() - 1
        for k in range(bits):
            if j & (1 << k):
                rev |= 1 << (bits - 1 - k)
        order.append(rev)
    all_back = gathered.reshape(col_devices * c_rows, nodes)
    out_order = jnp.array(
        [order[j] * c_rows + k for j in range(col_devices) for k in range(c_rows)], jnp.int32
    )
    rows_in_order = jnp.take(my_rows, out_order, axis=1)

    hidden_back = jnp.einsum("hc,cn->hn", rows_in_order, all_back, preferred_element_type=jnp.float32)
    block_grad = jnp.einsum("hn,cn->hc", hidden_act, all_back, preferred_element_type=jnp.float32)
    inverse = [0] * (col_devices * c_rows)
    for pos in range(col_devices * c_rows):
        inverse[int(order[pos // c_rows]) * c_rows + pos % c_rows] = pos
    second_part = jnp.take(block_grad, jnp.array(inverse, jnp.int32), axis=1)

    sigmoid_val = jax.nn.sigmoid(hidden_sum)
    slope_back = (hidden_back * sigmoid_val * (1.0 + hidden_sum * (1.0 - sigmoid_val))).astype(
        jnp.bfloat16
    )
    first_part = jnp.einsum(
        "in,hn->ih", feat_sum, slope_back.astype(jnp.float32), precision=HI
    )

    class_sent = {}
    for e in shifts():
        reader = jnp.mod(me + e, row_devices)
        wanted = reading_blocks(long_sources, reader, me)
        parts = [block(class_in, b) for b in wanted]
        if e == 1:
            parts.append(class_in[:, nodes - BLK:])
        if e == -1:
            parts.append(class_in[:, :BLK])
        class_sent[e] = send_by(jnp.concatenate(parts, 0), "row", e)
    cls_pool = jnp.stack(
        [class_sent[e][q * c_rows:(q + 1) * c_rows] for e in shifts() for q in range(2)], 0
    )
    cls_panels = jnp.take(cls_pool, read_index, axis=0)
    scores = forward_sum(
        class_in.reshape(c_rows, NB, BLK),
        class_sent[1][2 * c_rows:],
        class_sent[-1][2 * c_rows:],
        cls_panels,
        band_blocks,
        long_blocks,
        targets,
    ).reshape(c_rows, nodes).astype(jnp.bfloat16)

    flat = jnp.concatenate([first_part.reshape(-1), second_part.reshape(-1)])
    for mask in [1, row_devices // 2] + [m for m in (2, 4, 8, 16, 32) if m < row_devices // 2]:
        if mask < row_devices:
            flat = flat + swap_with(flat, "row", mask)
    first_grad = flat[: first_part.size].reshape(first_part.shape)
    second_grad = flat[first_part.size:].reshape(second_part.shape)
    return (scores, first_grad, second_grad)


def solution(mesh):
    return jax.shard_map(
        local,
        mesh=mesh,
        in_specs=(
            P(None, "row"),
            P(None, "col"),
            P(),
            P("col", "row"),
            P("row", None, None, None),
            P("row", None, None),
            P("row", None),
            P(),
            P(),
        ),
        out_specs=(P("col", "row"), P(None, "col"), P("col", None)),
        check_vma=False,
    )
```

```python
import jax
import jax.numpy as jnp
from jax import lax
from jax.sharding import PartitionSpec as P

BLK = 128
NB = 16
REACH = 3
SLOTS = 12
HI = lax.Precision.HIGHEST


def shifts():
    return [e for e in range(-REACH, REACH + 1) if e != 0]


def shift_index(e):
    return e + REACH if e < 0 else e + REACH - 1


def send_by(x, axis, by):
    devices = lax.axis_size(axis)
    return lax.ppermute(x, axis, [(i, (i + by) % devices) for i in range(devices)])


def swap_with(x, axis, mask):
    devices = lax.axis_size(axis)
    return lax.ppermute(x, axis, [(i, i ^ mask) for i in range(devices)])


def slot_tables(long_sources, me, row_devices):
    steps = jnp.array(shifts(), jnp.int32)
    partners = jnp.concatenate([jnp.mod(me + steps, row_devices), jnp.mod(me - steps, row_devices)])
    rows = jnp.take(long_sources, partners, axis=0)
    hit = (rows // NB) == me
    earlier = jnp.arange(SLOTS)[None, :] < jnp.arange(SLOTS)[:, None]
    rank = jnp.sum((hit[:, None, :] & earlier[None]).astype(jnp.int32), axis=2)
    local = rows % NB
    picks = [jnp.sum(jnp.where(hit & (rank == q), local, 0), axis=1) for q in range(2)]
    table = jnp.stack(picks, 1)
    return table[: len(shifts())], table[len(shifts()):]


def own_slot_pairs(long_sources, me, row_devices):
    source = lax.dynamic_index_in_dim(long_sources, me, 0, keepdims=False)
    owner = source // NB
    offset = jnp.mod(owner - me, row_devices)
    offset = jnp.where(offset > row_devices // 2, offset - row_devices, offset)
    same = (owner[:, None] == owner[None, :]) & (
        jnp.arange(SLOTS)[None, :] < jnp.arange(SLOTS)[:, None]
    )
    rank = jnp.sum(same.astype(jnp.int32), axis=1)
    send_position = jnp.where(offset < 0, offset + REACH, offset + REACH - 1)
    read_position = jnp.where(offset > 0, -offset + REACH, -offset + REACH - 1)
    return send_position * 2 + rank, read_position * 2 + rank


def inverse_of(pairs):
    return jnp.sum(
        jnp.where(pairs[None, :] == jnp.arange(SLOTS)[:, None], jnp.arange(SLOTS)[None, :], 0), axis=1
    )


def forward_sum(blocks, prev_edge, next_edge, panels, band_blocks, long_in_order, targets_in_order):
    earlier = jnp.concatenate([prev_edge[:, None], blocks[:, :-1]], 1)
    onward = jnp.concatenate([blocks[:, 1:], next_edge[:, None]], 1)
    near = jnp.einsum("fbm,bnm->fbn", earlier, band_blocks[:, 0], preferred_element_type=jnp.float32)
    near = near + jnp.einsum("fbm,bnm->fbn", blocks, band_blocks[:, 1], preferred_element_type=jnp.float32)
    near = near + jnp.einsum("fbm,bnm->fbn", onward, band_blocks[:, 2], preferred_element_type=jnp.float32)
    contrib = jnp.einsum("kfm,knm->kfn", panels, long_in_order, preferred_element_type=jnp.float32)
    far = jnp.einsum("kb,kfn->fbn", targets_in_order, contrib, precision=HI)
    return near + far


def local(
    features,
    weight_in,
    weight_out,
    score_grad,
    band_blocks,
    long_blocks,
    long_rows,
    long_sources,
    long_counts,
):
    row_devices = lax.axis_size("row")
    col_devices = lax.axis_size("col")
    me = lax.axis_index("row")
    col_index = lax.axis_index("col")
    row_ids = long_rows[0]
    hidden_count = weight_in.shape[1]
    class_count = score_grad.shape[0]
    nodes = features.shape[1]
    h_rows = hidden_count
    f_rows = features.shape[0]
    c_rows = class_count
    hf_rows = h_rows + f_rows
    up = shift_index(1)
    down = shift_index(-1)

    live_count = lax.dynamic_index_in_dim(long_counts, me, 0, keepdims=False)
    is_live = jnp.arange(SLOTS, dtype=jnp.int32) < live_count
    live = is_live.astype(jnp.float32)
    targets = (
        (row_ids[:, None] == jnp.arange(NB, dtype=jnp.int32)[None, :]) & is_live[:, None]
    ).astype(jnp.float32)
    send_pair, read_pair = own_slot_pairs(long_sources, me, row_devices)
    sending_slot = inverse_of(send_pair)
    reading_slot = inverse_of(read_pair)
    long_read = jnp.take(long_blocks, reading_slot, axis=0)
    targets_read = jnp.take(targets, reading_slot, axis=0)
    wanted, landing_blocks = slot_tables(long_sources, me, row_devices)
    edge_block = jnp.array([[NB - 1 if e == 1 else 0] for e in shifts()], jnp.int32)
    pick = jnp.concatenate([wanted, edge_block], 1).reshape(-1)

    hidden_in = jnp.einsum(
        "ih,in->hn", weight_in, features, preferred_element_type=jnp.float32
    ).astype(jnp.bfloat16)
    both_in = jnp.concatenate([hidden_in, features], 0)
    both_blocks = both_in.reshape(hf_rows, NB, BLK)

    sg_blocks = score_grad.reshape(class_count, NB, BLK)
    sg_prior = jnp.einsum("fbn,bnm->fbm", sg_blocks, band_blocks[:, 0], preferred_element_type=jnp.float32)
    sg_middle = jnp.einsum("fbn,bnm->fbm", sg_blocks, band_blocks[:, 1], preferred_element_type=jnp.float32)
    sg_later = jnp.einsum("fbn,bnm->fbm", sg_blocks, band_blocks[:, 2], preferred_element_type=jnp.float32)
    sg_rows = jnp.take(sg_blocks, jnp.take(row_ids, sending_slot), axis=1)
    sg_out = jnp.einsum(
        "fkn,knm->kfm", sg_rows, jnp.take(long_blocks, sending_slot, axis=0),
        preferred_element_type=jnp.float32,
    )
    sg_out = sg_out * jnp.take(live, sending_slot)[:, None, None]
    sg_edges = jnp.zeros((len(shifts()), 1, c_rows, BLK), jnp.float32)
    sg_edges = sg_edges.at[up, 0].set(sg_later[:, NB - 1]).at[down, 0].set(sg_prior[:, 0])
    sg_send = jnp.concatenate([sg_out.reshape(len(shifts()), 2, c_rows, BLK), sg_edges], 1)

    picked = jnp.take(both_blocks.transpose(1, 0, 2), pick, axis=0)
    picked = picked.reshape(len(shifts()), 3, hf_rows, BLK).astype(jnp.float32)
    send_all = jnp.concatenate([picked, sg_send], 2)
    arrived = [send_by(send_all[i], "row", e) for i, e in enumerate(shifts())]
    pairs_in = jnp.concatenate([a[:2] for a in arrived], 0)

    both_sum = forward_sum(
        both_blocks,
        arrived[up][2, :hf_rows].astype(jnp.bfloat16),
        arrived[down][2, :hf_rows].astype(jnp.bfloat16),
        pairs_in[:, :hf_rows].astype(jnp.bfloat16),
        band_blocks,
        long_read,
        targets_read,
    )
    hidden_sum = both_sum[:h_rows].reshape(h_rows, nodes)
    feat_sum = both_sum[h_rows:].reshape(f_rows, nodes)

    landing = (
        landing_blocks.reshape(-1)[:, None] == jnp.arange(NB, dtype=jnp.int32)[None, :]
    ).astype(jnp.float32)
    sg_sum = (
        sg_middle
        + jnp.concatenate([sg_prior[:, 1:], arrived[down][2, hf_rows:][:, None]], 1)
        + jnp.concatenate([arrived[up][2, hf_rows:][:, None], sg_later[:, :-1]], 1)
        + jnp.einsum("kb,kfm->fbm", landing, pairs_in[:, hf_rows:], precision=HI)
    )
    class_back = sg_sum.reshape(c_rows, nodes).astype(jnp.bfloat16)

    hidden_act = jax.nn.silu(hidden_sum).astype(jnp.bfloat16)

    my_rows = lax.dynamic_slice_in_dim(weight_out, col_index * hidden_count, hidden_count, 0)
    class_part = jnp.einsum("hc,hn->cn", my_rows, hidden_act, preferred_element_type=jnp.float32)
    reduced = class_part.reshape(col_devices, c_rows, nodes)
    gathered = class_back.reshape(1, c_rows, nodes)
    mask = col_devices // 2
    while mask >= 1:
        bit = (col_index // mask) % 2
        halves = reduced.reshape(2, -1, c_rows, nodes)
        keep = lax.dynamic_index_in_dim(halves, bit, 0, keepdims=False)
        away = lax.dynamic_index_in_dim(halves, 1 - bit, 0, keepdims=False)
        count = away.shape[0]
        both = swap_with(jnp.concatenate([away, gathered.astype(jnp.float32)], 0), "col", mask)
        reduced = keep + both[:count]
        other = both[count:].astype(jnp.bfloat16)
        gathered = jnp.where(
            bit == 0,
            jnp.concatenate([gathered, other], 0),
            jnp.concatenate([other, gathered], 0),
        )
        mask //= 2
    class_in = reduced.reshape(c_rows, nodes).astype(jnp.bfloat16)
    order = []
    for j in range(col_devices):
        rev = 0
        bits = col_devices.bit_length() - 1
        for k in range(bits):
            if j & (1 << k):
                rev |= 1 << (bits - 1 - k)
        order.append(rev)
    all_back = gathered.reshape(col_devices * c_rows, nodes)
    out_order = jnp.array(
        [order[j] * c_rows + k for j in range(col_devices) for k in range(c_rows)], jnp.int32
    )
    rows_in_order = jnp.take(my_rows, out_order, axis=1)

    hidden_back = jnp.einsum("hc,cn->hn", rows_in_order, all_back, preferred_element_type=jnp.float32)
    block_grad = jnp.einsum("hn,cn->hc", hidden_act, all_back, preferred_element_type=jnp.float32)
    inverse = [0] * (col_devices * c_rows)
    for pos in range(col_devices * c_rows):
        inverse[int(order[pos // c_rows]) * c_rows + pos % c_rows] = pos
    second_part = jnp.take(block_grad, jnp.array(inverse, jnp.int32), axis=1)

    sigmoid_val = jax.nn.sigmoid(hidden_sum)
    slope_back = (hidden_back * sigmoid_val * (1.0 + hidden_sum * (1.0 - sigmoid_val))).astype(
        jnp.bfloat16
    )
    first_part = jnp.einsum(
        "in,hn->ih", feat_sum, slope_back.astype(jnp.float32), precision=HI
    )

    class_blocks = class_in.reshape(c_rows, NB, BLK)
    class_pick = jnp.take(class_blocks.transpose(1, 0, 2), pick, axis=0)
    class_pick = class_pick.reshape(len(shifts()), 3, c_rows, BLK)
    class_arrived = [send_by(class_pick[i], "row", e) for i, e in enumerate(shifts())]
    class_pairs = jnp.concatenate([a[:2] for a in class_arrived], 0)
    scores = forward_sum(
        class_blocks,
        class_arrived[up][2],
        class_arrived[down][2],
        class_pairs,
        band_blocks,
        long_read,
        targets_read,
    ).reshape(c_rows, nodes).astype(jnp.bfloat16)

    flat = jnp.concatenate([first_part.reshape(-1), second_part.reshape(-1)])
    for mask in [1, row_devices // 2] + [m for m in (2, 4, 8, 16, 32) if m < row_devices // 2]:
        if mask < row_devices:
            flat = flat + swap_with(flat, "row", mask)
    first_grad = flat[: first_part.size].reshape(first_part.shape)
    second_grad = flat[first_part.size:].reshape(second_part.shape)
    return (scores, first_grad, second_grad)


def solution(mesh):
    return jax.shard_map(
        local,
        mesh=mesh,
        in_specs=(
            P(None, "row"),
            P(None, "col"),
            P(),
            P("col", "row"),
            P("row", None, None, None),
            P("row", None, None),
            P("row", None),
            P(),
            P(),
        ),
        out_specs=(P("col", "row"), P(None, "col"), P("col", None)),
        check_vma=False,
    )
```

```python
import jax
import jax.numpy as jnp
from jax import lax
from jax.sharding import PartitionSpec as P

BLK = 128
NB = 16
REACH = 3
SLOTS = 12
HI = lax.Precision.HIGHEST


def shifts():
    return [e for e in range(-REACH, REACH + 1) if e != 0]


def shift_index(e):
    return e + REACH if e < 0 else e + REACH - 1


def send_by(x, axis, by):
    devices = lax.axis_size(axis)
    return lax.ppermute(x, axis, [(i, (i + by) % devices) for i in range(devices)])


def swap_with(x, axis, mask):
    devices = lax.axis_size(axis)
    return lax.ppermute(x, axis, [(i, i ^ mask) for i in range(devices)])


def slot_tables(long_sources, me, row_devices):
    steps = jnp.array(shifts(), jnp.int32)
    partners = jnp.concatenate([jnp.mod(me + steps, row_devices), jnp.mod(me - steps, row_devices)])
    rows = jnp.take(long_sources, partners, axis=0)
    hit = (rows // NB) == me
    earlier = jnp.arange(SLOTS)[None, :] < jnp.arange(SLOTS)[:, None]
    rank = jnp.sum((hit[:, None, :] & earlier[None]).astype(jnp.int32), axis=2)
    local = rows % NB
    picks = [jnp.sum(jnp.where(hit & (rank == q), local, 0), axis=1) for q in range(2)]
    table = jnp.stack(picks, 1)
    return table[: len(shifts())], table[len(shifts()):]


def own_slot_pairs(long_sources, me, row_devices):
    source = lax.dynamic_index_in_dim(long_sources, me, 0, keepdims=False)
    owner = source // NB
    offset = jnp.mod(owner - me, row_devices)
    offset = jnp.where(offset > row_devices // 2, offset - row_devices, offset)
    same = (owner[:, None] == owner[None, :]) & (
        jnp.arange(SLOTS)[None, :] < jnp.arange(SLOTS)[:, None]
    )
    rank = jnp.sum(same.astype(jnp.int32), axis=1)
    send_position = jnp.where(offset < 0, offset + REACH, offset + REACH - 1)
    read_position = jnp.where(offset > 0, -offset + REACH, -offset + REACH - 1)
    return send_position * 2 + rank, read_position * 2 + rank


def inverse_of(pairs):
    return jnp.sum(
        jnp.where(pairs[None, :] == jnp.arange(SLOTS)[:, None], jnp.arange(SLOTS)[None, :], 0), axis=1
    )


def forward_sum(blocks, prev_edge, next_edge, panels, band_blocks, long_in_order, targets_in_order):
    earlier = jnp.concatenate([prev_edge[:, None], blocks[:, :-1]], 1)
    onward = jnp.concatenate([blocks[:, 1:], next_edge[:, None]], 1)
    near = jnp.einsum("fbm,bnm->fbn", earlier, band_blocks[:, 0], preferred_element_type=jnp.float32)
    near = near + jnp.einsum("fbm,bnm->fbn", blocks, band_blocks[:, 1], preferred_element_type=jnp.float32)
    near = near + jnp.einsum("fbm,bnm->fbn", onward, band_blocks[:, 2], preferred_element_type=jnp.float32)
    contrib = jnp.einsum("kfm,knm->kfn", panels, long_in_order, preferred_element_type=jnp.float32)
    far = jnp.einsum("kb,kfn->fbn", targets_in_order, contrib, precision=HI)
    return near + far


def local(
    features,
    weight_in,
    weight_out,
    score_grad,
    band_blocks,
    long_blocks,
    long_rows,
    long_sources,
    long_counts,
):
    row_devices = lax.axis_size("row")
    col_devices = lax.axis_size("col")
    me = lax.axis_index("row")
    col_index = lax.axis_index("col")
    row_ids = long_rows[0]
    hidden_count = weight_in.shape[1]
    class_count = score_grad.shape[0]
    nodes = features.shape[1]
    h_rows = hidden_count
    f_rows = features.shape[0]
    c_rows = class_count
    hf_rows = h_rows + f_rows
    up = shift_index(1)
    down = shift_index(-1)

    live_count = lax.dynamic_index_in_dim(long_counts, me, 0, keepdims=False)
    is_live = jnp.arange(SLOTS, dtype=jnp.int32) < live_count
    live = is_live.astype(jnp.float32)
    targets = (
        (row_ids[:, None] == jnp.arange(NB, dtype=jnp.int32)[None, :]) & is_live[:, None]
    ).astype(jnp.float32)
    send_pair, read_pair = own_slot_pairs(long_sources, me, row_devices)
    sending_slot = inverse_of(send_pair)
    reading_slot = inverse_of(read_pair)
    long_read = jnp.take(long_blocks, reading_slot, axis=0)
    targets_read = jnp.take(targets, reading_slot, axis=0)
    wanted, landing_blocks = slot_tables(long_sources, me, row_devices)
    edge_block = jnp.array([[NB - 1 if e == 1 else 0] for e in shifts()], jnp.int32)
    pick = jnp.concatenate([wanted, edge_block], 1).reshape(-1)

    hidden_in = jnp.einsum(
        "ih,in->hn", weight_in, features, preferred_element_type=jnp.float32
    ).astype(jnp.bfloat16)
    both_in = jnp.concatenate([hidden_in, features], 0)
    both_blocks = both_in.reshape(hf_rows, NB, BLK)

    sg_blocks = score_grad.reshape(class_count, NB, BLK)
    sg_prior = jnp.einsum("fbn,bnm->fbm", sg_blocks, band_blocks[:, 0], preferred_element_type=jnp.float32)
    sg_middle = jnp.einsum("fbn,bnm->fbm", sg_blocks, band_blocks[:, 1], preferred_element_type=jnp.float32)
    sg_later = jnp.einsum("fbn,bnm->fbm", sg_blocks, band_blocks[:, 2], preferred_element_type=jnp.float32)
    sg_rows = jnp.take(sg_blocks, jnp.take(row_ids, sending_slot), axis=1)
    sg_out = jnp.einsum(
        "fkn,knm->kfm", sg_rows, jnp.take(long_blocks, sending_slot, axis=0),
        preferred_element_type=jnp.float32,
    )
    sg_out = sg_out * jnp.take(live, sending_slot)[:, None, None]
    sg_edges = jnp.zeros((len(shifts()), 1, c_rows, BLK), jnp.float32)
    sg_edges = sg_edges.at[up, 0].set(sg_later[:, NB - 1]).at[down, 0].set(sg_prior[:, 0])
    sg_send = jnp.concatenate([sg_out.reshape(len(shifts()), 2, c_rows, BLK), sg_edges], 1)

    picked = jnp.take(both_blocks.transpose(1, 0, 2), pick, axis=0)
    picked = picked.reshape(len(shifts()), 3, hf_rows, BLK).astype(jnp.float32)
    send_all = jnp.concatenate([picked, sg_send], 2)
    arrived = [send_by(send_all[i], "row", e) for i, e in enumerate(shifts())]
    pairs_in = jnp.concatenate([a[:2] for a in arrived], 0)

    both_sum = forward_sum(
        both_blocks,
        arrived[up][2, :hf_rows].astype(jnp.bfloat16),
        arrived[down][2, :hf_rows].astype(jnp.bfloat16),
        pairs_in[:, :hf_rows].astype(jnp.bfloat16),
        band_blocks,
        long_read,
        targets_read,
    )
    hidden_sum = both_sum[:h_rows].reshape(h_rows, nodes)
    feat_sum = both_sum[h_rows:].reshape(f_rows, nodes)

    landing = (
        landing_blocks.reshape(-1)[:, None] == jnp.arange(NB, dtype=jnp.int32)[None, :]
    ).astype(jnp.float32)
    sg_sum = (
        sg_middle
        + jnp.concatenate([sg_prior[:, 1:], arrived[down][2, hf_rows:][:, None]], 1)
        + jnp.concatenate([arrived[up][2, hf_rows:][:, None], sg_later[:, :-1]], 1)
        + jnp.einsum("kb,kfm->fbm", landing, pairs_in[:, hf_rows:], precision=HI)
    )
    class_back = sg_sum.reshape(c_rows, nodes).astype(jnp.bfloat16)

    hidden_act = jax.nn.silu(hidden_sum).astype(jnp.bfloat16)

    my_rows = lax.dynamic_slice_in_dim(weight_out, col_index * hidden_count, hidden_count, 0)
    class_part = jnp.einsum("hc,hn->cn", my_rows, hidden_act, preferred_element_type=jnp.float32)
    part_blocks = class_part.reshape(col_devices, c_rows, nodes)
    xor_order = jnp.bitwise_xor(col_index, jnp.arange(col_devices, dtype=jnp.int32))
    away = jnp.take(part_blocks, xor_order[1:], axis=0)
    mine = jnp.broadcast_to(class_back.astype(jnp.float32)[None], away.shape)
    outgoing = jnp.stack([away, mine], 1)
    incoming = [swap_with(outgoing[m - 1], "col", m) for m in range(1, col_devices)]
    own_part = lax.dynamic_index_in_dim(part_blocks, col_index, 0, keepdims=False)
    class_in = (own_part + sum(x[0] for x in incoming)).astype(jnp.bfloat16)
    all_back = jnp.concatenate(
        [class_back] + [x[1].astype(jnp.bfloat16) for x in incoming], 0
    )
    rows_in_order = jnp.take(
        my_rows.reshape(hidden_count, col_devices, c_rows), xor_order, axis=1
    ).reshape(hidden_count, col_devices * c_rows)

    hidden_back = jnp.einsum("hc,cn->hn", rows_in_order, all_back, preferred_element_type=jnp.float32)
    block_grad = jnp.einsum("hn,cn->hc", hidden_act, all_back, preferred_element_type=jnp.float32)
    second_part = jnp.take(
        block_grad.reshape(hidden_count, col_devices, c_rows), xor_order, axis=1
    ).reshape(hidden_count, col_devices * c_rows)

    sigmoid_val = jax.nn.sigmoid(hidden_sum)
    slope_back = (hidden_back * sigmoid_val * (1.0 + hidden_sum * (1.0 - sigmoid_val))).astype(
        jnp.bfloat16
    )
    first_part = jnp.einsum(
        "in,hn->ih", feat_sum, slope_back.astype(jnp.float32), precision=HI
    )

    class_blocks = class_in.reshape(c_rows, NB, BLK)
    class_pick = jnp.take(class_blocks.transpose(1, 0, 2), pick, axis=0)
    class_pick = class_pick.reshape(len(shifts()), 3, c_rows, BLK)
    class_arrived = [send_by(class_pick[i], "row", e) for i, e in enumerate(shifts())]
    class_pairs = jnp.concatenate([a[:2] for a in class_arrived], 0)
    scores = forward_sum(
        class_blocks,
        class_arrived[up][2],
        class_arrived[down][2],
        class_pairs,
        band_blocks,
        long_read,
        targets_read,
    ).reshape(c_rows, nodes).astype(jnp.bfloat16)

    flat = jnp.concatenate([first_part.reshape(-1), second_part.reshape(-1)])
    for mask in [1, row_devices // 2] + [m for m in (2, 4, 8, 16, 32) if m < row_devices // 2]:
        if mask < row_devices:
            flat = flat + swap_with(flat, "row", mask)
    first_grad = flat[: first_part.size].reshape(first_part.shape)
    second_grad = flat[first_part.size:].reshape(second_part.shape)
    return (scores, first_grad, second_grad)


def solution(mesh):
    return jax.shard_map(
        local,
        mesh=mesh,
        in_specs=(
            P(None, "row"),
            P(None, "col"),
            P(),
            P("col", "row"),
            P("row", None, None, None),
            P("row", None, None),
            P("row", None),
            P(),
            P(),
        ),
        out_specs=(P("col", "row"), P(None, "col"), P("col", None)),
        check_vma=False,
    )
```

```python
import jax
import jax.numpy as jnp
from jax import lax
from jax.sharding import PartitionSpec as P

BLK = 128
NB = 16
REACH = 3
SLOTS = 12
HI = lax.Precision.HIGHEST


def shifts():
    return [e for e in range(-REACH, REACH + 1) if e != 0]


def shift_index(e):
    return e + REACH if e < 0 else e + REACH - 1


def send_by(x, axis, by):
    devices = lax.axis_size(axis)
    return lax.ppermute(x, axis, [(i, (i + by) % devices) for i in range(devices)])


def swap_with(x, axis, mask):
    devices = lax.axis_size(axis)
    return lax.ppermute(x, axis, [(i, i ^ mask) for i in range(devices)])


def slot_tables(long_sources, me, row_devices):
    steps = jnp.array(shifts(), jnp.int32)
    partners = jnp.concatenate([jnp.mod(me + steps, row_devices), jnp.mod(me - steps, row_devices)])
    rows = jnp.take(long_sources, partners, axis=0)
    hit = (rows // NB) == me
    earlier = jnp.arange(SLOTS)[None, :] < jnp.arange(SLOTS)[:, None]
    rank = jnp.sum((hit[:, None, :] & earlier[None]).astype(jnp.int32), axis=2)
    local = rows % NB
    picks = [jnp.sum(jnp.where(hit & (rank == q), local, 0), axis=1) for q in range(2)]
    table = jnp.stack(picks, 1)
    return table[: len(shifts())], table[len(shifts()):]


def own_slot_pairs(long_sources, me, row_devices):
    source = lax.dynamic_index_in_dim(long_sources, me, 0, keepdims=False)
    owner = source // NB
    offset = jnp.mod(owner - me, row_devices)
    offset = jnp.where(offset > row_devices // 2, offset - row_devices, offset)
    same = (owner[:, None] == owner[None, :]) & (
        jnp.arange(SLOTS)[None, :] < jnp.arange(SLOTS)[:, None]
    )
    rank = jnp.sum(same.astype(jnp.int32), axis=1)
    send_position = jnp.where(offset < 0, offset + REACH, offset + REACH - 1)
    read_position = jnp.where(offset > 0, -offset + REACH, -offset + REACH - 1)
    return send_position * 2 + rank, read_position * 2 + rank


def inverse_of(pairs):
    return jnp.sum(
        jnp.where(pairs[None, :] == jnp.arange(SLOTS)[:, None], jnp.arange(SLOTS)[None, :], 0), axis=1
    )


def forward_sum(blocks, prev_edge, next_edge, panels, band_blocks, long_in_order, targets_in_order):
    earlier = jnp.concatenate([prev_edge[:, None], blocks[:, :-1]], 1)
    onward = jnp.concatenate([blocks[:, 1:], next_edge[:, None]], 1)
    near = jnp.einsum("fbm,bnm->fbn", earlier, band_blocks[:, 0], preferred_element_type=jnp.float32)
    near = near + jnp.einsum("fbm,bnm->fbn", blocks, band_blocks[:, 1], preferred_element_type=jnp.float32)
    near = near + jnp.einsum("fbm,bnm->fbn", onward, band_blocks[:, 2], preferred_element_type=jnp.float32)
    contrib = jnp.einsum("kfm,knm->kfn", panels, long_in_order, preferred_element_type=jnp.float32)
    far = jnp.einsum("kb,kfn->fbn", targets_in_order, contrib, precision=HI)
    return near + far


def local(
    features,
    weight_in,
    weight_out,
    score_grad,
    band_blocks,
    long_blocks,
    long_rows,
    long_sources,
    long_counts,
):
    row_devices = lax.axis_size("row")
    col_devices = lax.axis_size("col")
    me = lax.axis_index("row")
    col_index = lax.axis_index("col")
    row_ids = long_rows[0]
    hidden_count = weight_in.shape[1]
    class_count = score_grad.shape[0]
    nodes = features.shape[1]
    h_rows = hidden_count
    f_rows = features.shape[0]
    c_rows = class_count
    hf_rows = h_rows + f_rows
    up = shift_index(1)
    down = shift_index(-1)

    live_count = lax.dynamic_index_in_dim(long_counts, me, 0, keepdims=False)
    is_live = jnp.arange(SLOTS, dtype=jnp.int32) < live_count
    live = is_live.astype(jnp.float32)
    targets = (
        (row_ids[:, None] == jnp.arange(NB, dtype=jnp.int32)[None, :]) & is_live[:, None]
    ).astype(jnp.float32)
    send_pair, read_pair = own_slot_pairs(long_sources, me, row_devices)
    sending_slot = inverse_of(send_pair)
    reading_slot = inverse_of(read_pair)
    long_read = jnp.take(long_blocks, reading_slot, axis=0)
    targets_read = jnp.take(targets, reading_slot, axis=0)
    wanted, landing_blocks = slot_tables(long_sources, me, row_devices)
    edge_block = jnp.array([[NB - 1 if e == 1 else 0] for e in shifts()], jnp.int32)
    pick = jnp.concatenate([wanted, edge_block], 1).reshape(-1)

    hidden_in = jnp.einsum(
        "ih,in->hn", weight_in, features, preferred_element_type=jnp.float32
    ).astype(jnp.bfloat16)
    both_in = jnp.concatenate([hidden_in, features], 0)
    both_blocks = both_in.reshape(hf_rows, NB, BLK)

    sg_blocks = score_grad.reshape(class_count, NB, BLK)
    sg_prior = jnp.einsum("fbn,bnm->fbm", sg_blocks, band_blocks[:, 0], preferred_element_type=jnp.float32)
    sg_middle = jnp.einsum("fbn,bnm->fbm", sg_blocks, band_blocks[:, 1], preferred_element_type=jnp.float32)
    sg_later = jnp.einsum("fbn,bnm->fbm", sg_blocks, band_blocks[:, 2], preferred_element_type=jnp.float32)
    sg_rows = jnp.take(sg_blocks, jnp.take(row_ids, sending_slot), axis=1)
    sg_out = jnp.einsum(
        "fkn,knm->kfm", sg_rows, jnp.take(long_blocks, sending_slot, axis=0),
        preferred_element_type=jnp.float32,
    )
    sg_out = sg_out * jnp.take(live, sending_slot)[:, None, None]
    sg_edges = jnp.zeros((len(shifts()), 1, c_rows, BLK), jnp.float32)
    sg_edges = sg_edges.at[up, 0].set(sg_later[:, NB - 1]).at[down, 0].set(sg_prior[:, 0])
    sg_send = jnp.concatenate([sg_out.reshape(len(shifts()), 2, c_rows, BLK), sg_edges], 1)

    picked = jnp.take(both_blocks.transpose(1, 0, 2), pick, axis=0)
    picked = picked.reshape(len(shifts()), 3, hf_rows, BLK).astype(jnp.float32)
    send_all = jnp.concatenate([picked, sg_send], 2)
    arrived = [send_by(send_all[i], "row", e) for i, e in enumerate(shifts())]
    pairs_in = jnp.concatenate([a[:2] for a in arrived], 0)

    both_sum = forward_sum(
        both_blocks,
        arrived[up][2, :hf_rows].astype(jnp.bfloat16),
        arrived[down][2, :hf_rows].astype(jnp.bfloat16),
        pairs_in[:, :hf_rows].astype(jnp.bfloat16),
        band_blocks,
        long_read,
        targets_read,
    )
    hidden_sum = both_sum[:h_rows].reshape(h_rows, nodes)
    feat_sum = both_sum[h_rows:].reshape(f_rows, nodes)

    landing = (
        landing_blocks.reshape(-1)[:, None] == jnp.arange(NB, dtype=jnp.int32)[None, :]
    ).astype(jnp.float32)
    sg_sum = (
        sg_middle
        + jnp.concatenate([sg_prior[:, 1:], arrived[down][2, hf_rows:][:, None]], 1)
        + jnp.concatenate([arrived[up][2, hf_rows:][:, None], sg_later[:, :-1]], 1)
        + jnp.einsum("kb,kfm->fbm", landing, pairs_in[:, hf_rows:], precision=HI)
    )
    class_back = sg_sum.reshape(c_rows, nodes).astype(jnp.bfloat16)

    hidden_act = jax.nn.silu(hidden_sum).astype(jnp.bfloat16)

    my_rows = lax.dynamic_slice_in_dim(weight_out, col_index * hidden_count, hidden_count, 0)
    class_part = jnp.einsum("hc,hn->cn", my_rows, hidden_act, preferred_element_type=jnp.float32)
    part_blocks = class_part.reshape(col_devices, c_rows, nodes)
    mine = jnp.broadcast_to(class_back.astype(jnp.float32)[None], part_blocks.shape)
    outgoing = jnp.stack([part_blocks, mine], 1)
    incoming = lax.all_to_all(outgoing, "col", 0, 0, tiled=True)
    class_in = jnp.sum(incoming[:, 0], axis=0).astype(jnp.bfloat16)
    all_back = incoming[:, 1].astype(jnp.bfloat16).reshape(col_devices * c_rows, nodes)

    hidden_back = jnp.einsum("hc,cn->hn", my_rows, all_back, preferred_element_type=jnp.float32)
    second_part = jnp.einsum("hn,cn->hc", hidden_act, all_back, preferred_element_type=jnp.float32)

    sigmoid_val = jax.nn.sigmoid(hidden_sum)
    slope_back = (hidden_back * sigmoid_val * (1.0 + hidden_sum * (1.0 - sigmoid_val))).astype(
        jnp.bfloat16
    )
    first_part = jnp.einsum(
        "in,hn->ih", feat_sum, slope_back.astype(jnp.float32), precision=HI
    )

    class_blocks = class_in.reshape(c_rows, NB, BLK)
    class_pick = jnp.take(class_blocks.transpose(1, 0, 2), pick, axis=0)
    class_pick = class_pick.reshape(len(shifts()), 3, c_rows, BLK)
    class_arrived = [send_by(class_pick[i], "row", e) for i, e in enumerate(shifts())]
    class_pairs = jnp.concatenate([a[:2] for a in class_arrived], 0)
    scores = forward_sum(
        class_blocks,
        class_arrived[up][2],
        class_arrived[down][2],
        class_pairs,
        band_blocks,
        long_read,
        targets_read,
    ).reshape(c_rows, nodes).astype(jnp.bfloat16)

    flat = jnp.concatenate([first_part.reshape(-1), second_part.reshape(-1)])
    for mask in [1, row_devices // 2] + [m for m in (2, 4, 8, 16, 32) if m < row_devices // 2]:
        if mask < row_devices:
            flat = flat + swap_with(flat, "row", mask)
    first_grad = flat[: first_part.size].reshape(first_part.shape)
    second_grad = flat[first_part.size:].reshape(second_part.shape)
    return (scores, first_grad, second_grad)


def solution(mesh):
    return jax.shard_map(
        local,
        mesh=mesh,
        in_specs=(
            P(None, "row"),
            P(None, "col"),
            P(),
            P("col", "row"),
            P("row", None, None, None),
            P("row", None, None),
            P("row", None),
            P(),
            P(),
        ),
        out_specs=(P("col", "row"), P(None, "col"), P("col", None)),
        check_vma=False,
    )
```

```python
import jax
import jax.numpy as jnp
from jax import lax
from jax.sharding import PartitionSpec as P

BLK = 128
NB = 16
REACH = 3
SLOTS = 12
HI = lax.Precision.HIGHEST


def shifts():
    return [e for e in range(-REACH, REACH + 1) if e != 0]


def shift_index(e):
    return e + REACH if e < 0 else e + REACH - 1


def send_by(x, axis, by):
    devices = lax.axis_size(axis)
    return lax.ppermute(x, axis, [(i, (i + by) % devices) for i in range(devices)])


def swap_with(x, axis, mask):
    devices = lax.axis_size(axis)
    return lax.ppermute(x, axis, [(i, i ^ mask) for i in range(devices)])


def slot_tables(long_sources, me, row_devices):
    steps = jnp.array(shifts(), jnp.int32)
    partners = jnp.concatenate([jnp.mod(me + steps, row_devices), jnp.mod(me - steps, row_devices)])
    rows = jnp.take(long_sources, partners, axis=0)
    hit = (rows // NB) == me
    earlier = jnp.arange(SLOTS)[None, :] < jnp.arange(SLOTS)[:, None]
    rank = jnp.sum((hit[:, None, :] & earlier[None]).astype(jnp.int32), axis=2)
    local = rows % NB
    picks = [jnp.sum(jnp.where(hit & (rank == q), local, 0), axis=1) for q in range(2)]
    table = jnp.stack(picks, 1)
    return table[: len(shifts())], table[len(shifts()):]


def own_slot_pairs(long_sources, me, row_devices):
    source = lax.dynamic_index_in_dim(long_sources, me, 0, keepdims=False)
    owner = source // NB
    offset = jnp.mod(owner - me, row_devices)
    offset = jnp.where(offset > row_devices // 2, offset - row_devices, offset)
    same = (owner[:, None] == owner[None, :]) & (
        jnp.arange(SLOTS)[None, :] < jnp.arange(SLOTS)[:, None]
    )
    rank = jnp.sum(same.astype(jnp.int32), axis=1)
    send_position = jnp.where(offset < 0, offset + REACH, offset + REACH - 1)
    read_position = jnp.where(offset > 0, -offset + REACH, -offset + REACH - 1)
    return send_position * 2 + rank, read_position * 2 + rank


def inverse_of(pairs):
    return jnp.sum(
        jnp.where(pairs[None, :] == jnp.arange(SLOTS)[:, None], jnp.arange(SLOTS)[None, :], 0), axis=1
    )


def forward_sum(blocks, prev_edge, next_edge, panels, band_blocks, long_in_order, targets_in_order):
    earlier = jnp.concatenate([prev_edge[:, None], blocks[:, :-1]], 1)
    onward = jnp.concatenate([blocks[:, 1:], next_edge[:, None]], 1)
    near = jnp.einsum("fbm,bnm->fbn", earlier, band_blocks[:, 0], preferred_element_type=jnp.float32)
    near = near + jnp.einsum("fbm,bnm->fbn", blocks, band_blocks[:, 1], preferred_element_type=jnp.float32)
    near = near + jnp.einsum("fbm,bnm->fbn", onward, band_blocks[:, 2], preferred_element_type=jnp.float32)
    contrib = jnp.einsum("kfm,knm->kfn", panels, long_in_order, preferred_element_type=jnp.float32)
    far = jnp.einsum("kb,kfn->fbn", targets_in_order, contrib, precision=HI)
    return near + far


def local(
    features,
    weight_in,
    weight_out,
    score_grad,
    band_blocks,
    long_blocks,
    long_rows,
    long_sources,
    long_counts,
):
    row_devices = lax.axis_size("row")
    col_devices = lax.axis_size("col")
    me = lax.axis_index("row")
    col_index = lax.axis_index("col")
    row_ids = long_rows[0]
    hidden_count = weight_in.shape[1]
    class_count = score_grad.shape[0]
    nodes = features.shape[1]
    h_rows = hidden_count
    f_rows = features.shape[0]
    c_rows = class_count
    hf_rows = h_rows + f_rows
    up = shift_index(1)
    down = shift_index(-1)

    live_count = lax.dynamic_index_in_dim(long_counts, me, 0, keepdims=False)
    is_live = jnp.arange(SLOTS, dtype=jnp.int32) < live_count
    live = is_live.astype(jnp.float32)
    targets = (
        (row_ids[:, None] == jnp.arange(NB, dtype=jnp.int32)[None, :]) & is_live[:, None]
    ).astype(jnp.float32)
    send_pair, read_pair = own_slot_pairs(long_sources, me, row_devices)
    sending_slot = inverse_of(send_pair)
    reading_slot = inverse_of(read_pair)
    long_read = jnp.take(long_blocks, reading_slot, axis=0)
    targets_read = jnp.take(targets, reading_slot, axis=0)
    wanted, landing_blocks = slot_tables(long_sources, me, row_devices)
    edge_block = jnp.array([[NB - 1 if e == 1 else 0] for e in shifts()], jnp.int32)
    pick = jnp.concatenate([wanted, edge_block], 1).reshape(-1)

    hidden_in = jnp.einsum(
        "ih,in->hn", weight_in, features, preferred_element_type=jnp.float32
    ).astype(jnp.bfloat16)
    both_in = jnp.concatenate([hidden_in, features], 0)
    both_blocks = both_in.reshape(hf_rows, NB, BLK)

    sg_blocks = score_grad.reshape(class_count, NB, BLK)
    sg_prior = jnp.einsum("fbn,bnm->fbm", sg_blocks, band_blocks[:, 0], preferred_element_type=jnp.float32)
    sg_middle = jnp.einsum("fbn,bnm->fbm", sg_blocks, band_blocks[:, 1], preferred_element_type=jnp.float32)
    sg_later = jnp.einsum("fbn,bnm->fbm", sg_blocks, band_blocks[:, 2], preferred_element_type=jnp.float32)
    sg_rows = jnp.take(sg_blocks, jnp.take(row_ids, sending_slot), axis=1)
    sg_out = jnp.einsum(
        "fkn,knm->kfm", sg_rows, jnp.take(long_blocks, sending_slot, axis=0),
        preferred_element_type=jnp.float32,
    )
    sg_out = sg_out * jnp.take(live, sending_slot)[:, None, None]
    sg_edges = jnp.zeros((len(shifts()), 1, c_rows, BLK), jnp.float32)
    sg_edges = sg_edges.at[up, 0].set(sg_later[:, NB - 1]).at[down, 0].set(sg_prior[:, 0])
    sg_send = jnp.concatenate([sg_out.reshape(len(shifts()), 2, c_rows, BLK), sg_edges], 1)

    picked = jnp.take(both_blocks.transpose(1, 0, 2), pick, axis=0)
    picked = picked.reshape(len(shifts()), 3, hf_rows, BLK).astype(jnp.float32)
    send_all = jnp.concatenate([picked, sg_send], 2)
    arrived = [send_by(send_all[i], "row", e) for i, e in enumerate(shifts())]
    pairs_in = jnp.concatenate([a[:2] for a in arrived], 0)

    both_sum = forward_sum(
        both_blocks,
        arrived[up][2, :hf_rows].astype(jnp.bfloat16),
        arrived[down][2, :hf_rows].astype(jnp.bfloat16),
        pairs_in[:, :hf_rows].astype(jnp.bfloat16),
        band_blocks,
        long_read,
        targets_read,
    )
    hidden_sum = both_sum[:h_rows].reshape(h_rows, nodes)
    feat_sum = both_sum[h_rows:].reshape(f_rows, nodes)

    landing = (
        landing_blocks.reshape(-1)[:, None] == jnp.arange(NB, dtype=jnp.int32)[None, :]
    ).astype(jnp.float32)
    sg_sum = (
        sg_middle
        + jnp.concatenate([sg_prior[:, 1:], arrived[down][2, hf_rows:][:, None]], 1)
        + jnp.concatenate([arrived[up][2, hf_rows:][:, None], sg_later[:, :-1]], 1)
        + jnp.einsum("kb,kfm->fbm", landing, pairs_in[:, hf_rows:], precision=HI)
    )
    class_back = sg_sum.reshape(c_rows, nodes).astype(jnp.bfloat16)

    hidden_act = jax.nn.silu(hidden_sum).astype(jnp.bfloat16)

    my_rows = lax.dynamic_slice_in_dim(weight_out, col_index * hidden_count, hidden_count, 0)
    class_part = jnp.einsum("hc,hn->cn", my_rows, hidden_act, preferred_element_type=jnp.float32)
    part_blocks = class_part.reshape(col_devices, c_rows, nodes)
    mine = jnp.broadcast_to(class_back.astype(jnp.float32)[None], part_blocks.shape)
    outgoing = jnp.stack([part_blocks, mine], 1)
    incoming = lax.all_to_all(outgoing, "col", 0, 0, tiled=True)
    class_in = jnp.sum(incoming[:, 0], axis=0).astype(jnp.bfloat16)
    all_back = incoming[:, 1].astype(jnp.bfloat16).reshape(col_devices * c_rows, nodes)

    hidden_back = jnp.einsum("hc,cn->hn", my_rows, all_back, preferred_element_type=jnp.float32)
    second_part = jnp.einsum("hn,cn->hc", hidden_act, all_back, preferred_element_type=jnp.float32)

    sigmoid_val = jax.nn.sigmoid(hidden_sum)
    slope_back = (hidden_back * sigmoid_val * (1.0 + hidden_sum * (1.0 - sigmoid_val))).astype(
        jnp.bfloat16
    )
    first_part = jnp.einsum(
        "in,hn->ih", feat_sum, slope_back.astype(jnp.float32), precision=HI
    )

    class_blocks = class_in.reshape(c_rows, NB, BLK)
    class_pick = jnp.take(class_blocks.transpose(1, 0, 2), pick, axis=0)
    class_pick = class_pick.reshape(len(shifts()), 3, c_rows, BLK)
    class_arrived = [send_by(class_pick[i], "row", e) for i, e in enumerate(shifts())]
    class_pairs = jnp.concatenate([a[:2] for a in class_arrived], 0)
    scores = forward_sum(
        class_blocks,
        class_arrived[up][2],
        class_arrived[down][2],
        class_pairs,
        band_blocks,
        long_read,
        targets_read,
    ).reshape(c_rows, nodes).astype(jnp.bfloat16)

    flat = jnp.concatenate([first_part.reshape(-1), second_part.reshape(-1)])
    pieces = lax.all_to_all(flat.reshape(row_devices, -1), "row", 0, 0, tiled=True)
    summed = jnp.sum(pieces, axis=0, keepdims=True)
    spread = jnp.broadcast_to(summed, (row_devices, summed.shape[1]))
    flat = lax.all_to_all(spread, "row", 0, 0, tiled=True).reshape(-1)
    first_grad = flat[: first_part.size].reshape(first_part.shape)
    second_grad = flat[first_part.size:].reshape(second_part.shape)
    return (scores, first_grad, second_grad)


def solution(mesh):
    return jax.shard_map(
        local,
        mesh=mesh,
        in_specs=(
            P(None, "row"),
            P(None, "col"),
            P(),
            P("col", "row"),
            P("row", None, None, None),
            P("row", None, None),
            P("row", None),
            P(),
            P(),
        ),
        out_specs=(P("col", "row"), P(None, "col"), P("col", None)),
        check_vma=False,
    )
```

```python
import jax
import jax.numpy as jnp
from jax import lax
from jax.sharding import PartitionSpec as P

BLK = 128
NB = 16
REACH = 3
SLOTS = 12
HI = lax.Precision.HIGHEST


def shifts():
    return [e for e in range(-REACH, REACH + 1) if e != 0]


def shift_index(e):
    return e + REACH if e < 0 else e + REACH - 1


def send_by(x, axis, by):
    devices = lax.axis_size(axis)
    return lax.ppermute(x, axis, [(i, (i + by) % devices) for i in range(devices)])


def swap_with(x, axis, mask):
    devices = lax.axis_size(axis)
    return lax.ppermute(x, axis, [(i, i ^ mask) for i in range(devices)])


def slot_tables(long_sources, me, row_devices):
    steps = jnp.array(shifts(), jnp.int32)
    partners = jnp.concatenate([jnp.mod(me + steps, row_devices), jnp.mod(me - steps, row_devices)])
    rows = jnp.take(long_sources, partners, axis=0)
    hit = (rows // NB) == me
    earlier = jnp.arange(SLOTS)[None, :] < jnp.arange(SLOTS)[:, None]
    rank = jnp.sum((hit[:, None, :] & earlier[None]).astype(jnp.int32), axis=2)
    local = rows % NB
    picks = [jnp.sum(jnp.where(hit & (rank == q), local, 0), axis=1) for q in range(2)]
    table = jnp.stack(picks, 1)
    return table[: len(shifts())], table[len(shifts()):]


def own_slot_pairs(long_sources, me, row_devices):
    source = lax.dynamic_index_in_dim(long_sources, me, 0, keepdims=False)
    owner = source // NB
    offset = jnp.mod(owner - me, row_devices)
    offset = jnp.where(offset > row_devices // 2, offset - row_devices, offset)
    same = (owner[:, None] == owner[None, :]) & (
        jnp.arange(SLOTS)[None, :] < jnp.arange(SLOTS)[:, None]
    )
    rank = jnp.sum(same.astype(jnp.int32), axis=1)
    send_position = jnp.where(offset < 0, offset + REACH, offset + REACH - 1)
    read_position = jnp.where(offset > 0, -offset + REACH, -offset + REACH - 1)
    return send_position * 2 + rank, read_position * 2 + rank


def inverse_of(pairs):
    return jnp.sum(
        jnp.where(pairs[None, :] == jnp.arange(SLOTS)[:, None], jnp.arange(SLOTS)[None, :], 0), axis=1
    )


def forward_sum(blocks, prev_edge, next_edge, panels, band_blocks, long_in_order, targets_in_order):
    earlier = jnp.concatenate([prev_edge[:, None], blocks[:, :-1]], 1)
    onward = jnp.concatenate([blocks[:, 1:], next_edge[:, None]], 1)
    near = jnp.einsum("fbm,bnm->fbn", earlier, band_blocks[:, 0], preferred_element_type=jnp.float32)
    near = near + jnp.einsum("fbm,bnm->fbn", blocks, band_blocks[:, 1], preferred_element_type=jnp.float32)
    near = near + jnp.einsum("fbm,bnm->fbn", onward, band_blocks[:, 2], preferred_element_type=jnp.float32)
    contrib = jnp.einsum("kfm,knm->kfn", panels, long_in_order, preferred_element_type=jnp.float32)
    far = jnp.einsum("kb,kfn->fbn", targets_in_order, contrib, precision=HI)
    return near + far


def local(
    features,
    weight_in,
    weight_out,
    score_grad,
    band_blocks,
    long_blocks,
    long_rows,
    long_sources,
    long_counts,
):
    row_devices = lax.axis_size("row")
    col_devices = lax.axis_size("col")
    me = lax.axis_index("row")
    col_index = lax.axis_index("col")
    row_ids = long_rows[0]
    hidden_count = weight_in.shape[1]
    class_count = score_grad.shape[0]
    nodes = features.shape[1]
    h_rows = hidden_count
    f_rows = features.shape[0]
    c_rows = class_count
    hf_rows = h_rows + f_rows
    up = shift_index(1)
    down = shift_index(-1)

    live_count = lax.dynamic_index_in_dim(long_counts, me, 0, keepdims=False)
    is_live = jnp.arange(SLOTS, dtype=jnp.int32) < live_count
    live = is_live.astype(jnp.float32)
    targets = (
        (row_ids[:, None] == jnp.arange(NB, dtype=jnp.int32)[None, :]) & is_live[:, None]
    ).astype(jnp.float32)
    send_pair, read_pair = own_slot_pairs(long_sources, me, row_devices)
    sending_slot = inverse_of(send_pair)
    reading_slot = inverse_of(read_pair)
    long_read = jnp.take(long_blocks, reading_slot, axis=0)
    targets_read = jnp.take(targets, reading_slot, axis=0)
    wanted, landing_blocks = slot_tables(long_sources, me, row_devices)
    edge_block = jnp.array([[NB - 1 if e == 1 else 0] for e in shifts()], jnp.int32)
    pick = jnp.concatenate([wanted, edge_block], 1).reshape(-1)

    hidden_in = jnp.einsum(
        "ih,in->hn", weight_in, features, preferred_element_type=jnp.float32
    ).astype(jnp.bfloat16)
    both_in = jnp.concatenate([hidden_in, features], 0)
    both_blocks = both_in.reshape(hf_rows, NB, BLK)

    sg_blocks = score_grad.reshape(class_count, NB, BLK)
    sg_prior = jnp.einsum("fbn,bnm->fbm", sg_blocks, band_blocks[:, 0], preferred_element_type=jnp.float32)
    sg_middle = jnp.einsum("fbn,bnm->fbm", sg_blocks, band_blocks[:, 1], preferred_element_type=jnp.float32)
    sg_later = jnp.einsum("fbn,bnm->fbm", sg_blocks, band_blocks[:, 2], preferred_element_type=jnp.float32)
    sg_rows = jnp.take(sg_blocks, jnp.take(row_ids, sending_slot), axis=1)
    sg_out = jnp.einsum(
        "fkn,knm->kfm", sg_rows, jnp.take(long_blocks, sending_slot, axis=0),
        preferred_element_type=jnp.float32,
    )
    sg_out = sg_out * jnp.take(live, sending_slot)[:, None, None]
    sg_edges = jnp.zeros((len(shifts()), 1, c_rows, BLK), jnp.float32)
    sg_edges = sg_edges.at[up, 0].set(sg_later[:, NB - 1]).at[down, 0].set(sg_prior[:, 0])
    sg_send = jnp.concatenate([sg_out.reshape(len(shifts()), 2, c_rows, BLK), sg_edges], 1)

    picked = jnp.take(both_blocks.transpose(1, 0, 2), pick, axis=0)
    picked = picked.reshape(len(shifts()), 3, hf_rows, BLK).astype(jnp.float32)
    send_all = jnp.concatenate([picked, sg_send], 2)
    arrived = [send_by(send_all[i], "row", e) for i, e in enumerate(shifts())]
    pairs_in = jnp.concatenate([a[:2] for a in arrived], 0)

    both_sum = forward_sum(
        both_blocks,
        arrived[up][2, :hf_rows].astype(jnp.bfloat16),
        arrived[down][2, :hf_rows].astype(jnp.bfloat16),
        pairs_in[:, :hf_rows].astype(jnp.bfloat16),
        band_blocks,
        long_read,
        targets_read,
    )
    hidden_sum = both_sum[:h_rows].reshape(h_rows, nodes)
    feat_sum = both_sum[h_rows:].reshape(f_rows, nodes)

    landing = (
        landing_blocks.reshape(-1)[:, None] == jnp.arange(NB, dtype=jnp.int32)[None, :]
    ).astype(jnp.float32)
    sg_sum = (
        sg_middle
        + jnp.concatenate([sg_prior[:, 1:], arrived[down][2, hf_rows:][:, None]], 1)
        + jnp.concatenate([arrived[up][2, hf_rows:][:, None], sg_later[:, :-1]], 1)
        + jnp.einsum("kb,kfm->fbm", landing, pairs_in[:, hf_rows:], precision=HI)
    )
    class_back = sg_sum.reshape(c_rows, nodes).astype(jnp.bfloat16)

    hidden_act = jax.nn.silu(hidden_sum).astype(jnp.bfloat16)

    my_rows = lax.dynamic_slice_in_dim(weight_out, col_index * hidden_count, hidden_count, 0)
    class_part = jnp.einsum("hc,hn->cn", my_rows, hidden_act, preferred_element_type=jnp.float32)
    part_blocks = class_part.reshape(col_devices, c_rows, nodes)
    mine = jnp.broadcast_to(class_back.astype(jnp.float32)[None], part_blocks.shape)
    outgoing = jnp.stack([part_blocks, mine], 1)
    incoming = lax.all_to_all(outgoing, "col", 0, 0, tiled=True)
    class_in = jnp.sum(incoming[:, 0], axis=0).astype(jnp.bfloat16)
    all_back = incoming[:, 1].astype(jnp.bfloat16).reshape(col_devices * c_rows, nodes)

    hidden_back = jnp.einsum("hc,cn->hn", my_rows, all_back, preferred_element_type=jnp.float32)
    second_part = jnp.einsum("hn,cn->hc", hidden_act, all_back, preferred_element_type=jnp.float32)

    sigmoid_val = jax.nn.sigmoid(hidden_sum)
    slope_back = (hidden_back * sigmoid_val * (1.0 + hidden_sum * (1.0 - sigmoid_val))).astype(
        jnp.bfloat16
    )
    first_part = jnp.einsum(
        "in,hn->ih", feat_sum, slope_back.astype(jnp.float32), precision=HI
    )

    class_blocks = class_in.reshape(c_rows, NB, BLK)
    class_pick = jnp.take(class_blocks.transpose(1, 0, 2), pick, axis=0)
    class_pick = class_pick.reshape(len(shifts()), 3, c_rows, BLK)
    lanes = jnp.zeros((row_devices,) + class_pick.shape[1:], class_pick.dtype)
    for i, e in enumerate(shifts()):
        lanes = lanes.at[e % row_devices].set(class_pick[i])
    doubled = jnp.concatenate([lanes, lanes], 0)
    outgoing = lax.dynamic_slice_in_dim(doubled, jnp.mod(row_devices - me, row_devices), row_devices, 0)
    incoming = lax.all_to_all(outgoing, "row", 0, 0, tiled=True)
    doubled = jnp.concatenate([incoming, incoming], 0)
    near = lax.dynamic_slice_in_dim(doubled, jnp.mod(me - REACH, row_devices), 2 * REACH + 1, 0)
    class_arrived = [near[REACH - e] for e in shifts()]
    class_pairs = jnp.concatenate([a[:2] for a in class_arrived], 0)
    scores = forward_sum(
        class_blocks,
        class_arrived[up][2],
        class_arrived[down][2],
        class_pairs,
        band_blocks,
        long_read,
        targets_read,
    ).reshape(c_rows, nodes).astype(jnp.bfloat16)

    flat = jnp.concatenate([first_part.reshape(-1), second_part.reshape(-1)])
    pieces = lax.all_to_all(flat.reshape(row_devices, -1), "row", 0, 0, tiled=True)
    summed = jnp.sum(pieces, axis=0, keepdims=True)
    spread = jnp.broadcast_to(summed, (row_devices, summed.shape[1]))
    flat = lax.all_to_all(spread, "row", 0, 0, tiled=True).reshape(-1)
    first_grad = flat[: first_part.size].reshape(first_part.shape)
    second_grad = flat[first_part.size:].reshape(second_part.shape)
    return (scores, first_grad, second_grad)


def solution(mesh):
    return jax.shard_map(
        local,
        mesh=mesh,
        in_specs=(
            P(None, "row"),
            P(None, "col"),
            P(),
            P("col", "row"),
            P("row", None, None, None),
            P("row", None, None),
            P("row", None),
            P(),
            P(),
        ),
        out_specs=(P("col", "row"), P(None, "col"), P("col", None)),
        check_vma=False,
    )
```

```python
import jax
import jax.numpy as jnp
from jax import lax
from jax.sharding import PartitionSpec as P

BLK = 128
NB = 16
REACH = 3
SLOTS = 12
HI = lax.Precision.HIGHEST


def shifts():
    return [e for e in range(-REACH, REACH + 1) if e != 0]


def shift_index(e):
    return e + REACH if e < 0 else e + REACH - 1


def send_by(x, axis, by):
    devices = lax.axis_size(axis)
    return lax.ppermute(x, axis, [(i, (i + by) % devices) for i in range(devices)])


def swap_with(x, axis, mask):
    devices = lax.axis_size(axis)
    return lax.ppermute(x, axis, [(i, i ^ mask) for i in range(devices)])


def slot_tables(long_sources, me, row_devices):
    steps = jnp.array(shifts(), jnp.int32)
    partners = jnp.concatenate([jnp.mod(me + steps, row_devices), jnp.mod(me - steps, row_devices)])
    rows = jnp.take(long_sources, partners, axis=0)
    hit = (rows // NB) == me
    earlier = jnp.arange(SLOTS)[None, :] < jnp.arange(SLOTS)[:, None]
    rank = jnp.sum((hit[:, None, :] & earlier[None]).astype(jnp.int32), axis=2)
    local = rows % NB
    picks = [jnp.sum(jnp.where(hit & (rank == q), local, 0), axis=1) for q in range(2)]
    table = jnp.stack(picks, 1)
    return table[: len(shifts())], table[len(shifts()):]


def own_slot_pairs(long_sources, me, row_devices):
    source = lax.dynamic_index_in_dim(long_sources, me, 0, keepdims=False)
    owner = source // NB
    offset = jnp.mod(owner - me, row_devices)
    offset = jnp.where(offset > row_devices // 2, offset - row_devices, offset)
    same = (owner[:, None] == owner[None, :]) & (
        jnp.arange(SLOTS)[None, :] < jnp.arange(SLOTS)[:, None]
    )
    rank = jnp.sum(same.astype(jnp.int32), axis=1)
    send_position = jnp.where(offset < 0, offset + REACH, offset + REACH - 1)
    read_position = jnp.where(offset > 0, -offset + REACH, -offset + REACH - 1)
    return send_position * 2 + rank, read_position * 2 + rank


def inverse_of(pairs):
    return jnp.sum(
        jnp.where(pairs[None, :] == jnp.arange(SLOTS)[:, None], jnp.arange(SLOTS)[None, :], 0), axis=1
    )


def forward_sum(blocks, prev_edge, next_edge, panels, band_blocks, long_in_order, targets_in_order):
    earlier = jnp.concatenate([prev_edge[:, None], blocks[:, :-1]], 1)
    onward = jnp.concatenate([blocks[:, 1:], next_edge[:, None]], 1)
    near = jnp.einsum("fbm,bnm->fbn", earlier, band_blocks[:, 0], preferred_element_type=jnp.float32)
    near = near + jnp.einsum("fbm,bnm->fbn", blocks, band_blocks[:, 1], preferred_element_type=jnp.float32)
    near = near + jnp.einsum("fbm,bnm->fbn", onward, band_blocks[:, 2], preferred_element_type=jnp.float32)
    contrib = jnp.einsum("kfm,knm->kfn", panels, long_in_order, preferred_element_type=jnp.float32)
    far = jnp.einsum("kb,kfn->fbn", targets_in_order, contrib, precision=HI)
    return near + far


def local(
    features,
    weight_in,
    weight_out,
    score_grad,
    band_blocks,
    long_blocks,
    long_rows,
    long_sources,
    long_counts,
):
    row_devices = lax.axis_size("row")
    col_devices = lax.axis_size("col")
    me = lax.axis_index("row")
    col_index = lax.axis_index("col")
    row_ids = long_rows[0]
    hidden_count = weight_in.shape[1]
    class_count = score_grad.shape[0]
    nodes = features.shape[1]
    h_rows = hidden_count
    f_rows = features.shape[0]
    c_rows = class_count
    hf_rows = h_rows + f_rows
    up = shift_index(1)
    down = shift_index(-1)

    live_count = lax.dynamic_index_in_dim(long_counts, me, 0, keepdims=False)
    is_live = jnp.arange(SLOTS, dtype=jnp.int32) < live_count
    live = is_live.astype(jnp.float32)
    targets = (
        (row_ids[:, None] == jnp.arange(NB, dtype=jnp.int32)[None, :]) & is_live[:, None]
    ).astype(jnp.float32)
    send_pair, read_pair = own_slot_pairs(long_sources, me, row_devices)
    sending_slot = inverse_of(send_pair)
    reading_slot = inverse_of(read_pair)
    long_read = jnp.take(long_blocks, reading_slot, axis=0)
    targets_read = jnp.take(targets, reading_slot, axis=0)
    wanted, landing_blocks = slot_tables(long_sources, me, row_devices)
    edge_block = jnp.array([[NB - 1 if e == 1 else 0] for e in shifts()], jnp.int32)
    pick = jnp.concatenate([wanted, edge_block], 1).reshape(-1)

    hidden_in = jnp.einsum(
        "ih,in->hn", weight_in, features, preferred_element_type=jnp.float32
    ).astype(jnp.bfloat16)
    both_in = jnp.concatenate([hidden_in, features], 0)
    both_blocks = both_in.reshape(hf_rows, NB, BLK)

    sg_blocks = score_grad.reshape(class_count, NB, BLK)
    sg_prior = jnp.einsum("fbn,bnm->fbm", sg_blocks, band_blocks[:, 0], preferred_element_type=jnp.float32)
    sg_middle = jnp.einsum("fbn,bnm->fbm", sg_blocks, band_blocks[:, 1], preferred_element_type=jnp.float32)
    sg_later = jnp.einsum("fbn,bnm->fbm", sg_blocks, band_blocks[:, 2], preferred_element_type=jnp.float32)
    sg_rows = jnp.take(sg_blocks, jnp.take(row_ids, sending_slot), axis=1)
    sg_out = jnp.einsum(
        "fkn,knm->kfm", sg_rows, jnp.take(long_blocks, sending_slot, axis=0),
        preferred_element_type=jnp.float32,
    )
    sg_out = sg_out * jnp.take(live, sending_slot)[:, None, None]
    sg_edges = jnp.zeros((len(shifts()), 1, c_rows, BLK), jnp.float32)
    sg_edges = sg_edges.at[up, 0].set(sg_later[:, NB - 1]).at[down, 0].set(sg_prior[:, 0])
    sg_send = jnp.concatenate([sg_out.reshape(len(shifts()), 2, c_rows, BLK), sg_edges], 1)

    picked = jnp.take(both_blocks.transpose(1, 0, 2), pick, axis=0)
    picked = picked.reshape(len(shifts()), 3, hf_rows, BLK).astype(jnp.float32)
    send_all = jnp.concatenate([picked, sg_send], 2)
    arrived = [send_by(send_all[i], "row", e) for i, e in enumerate(shifts())]
    pairs_in = jnp.concatenate([a[:2] for a in arrived], 0)

    both_sum = forward_sum(
        both_blocks,
        arrived[up][2, :hf_rows].astype(jnp.bfloat16),
        arrived[down][2, :hf_rows].astype(jnp.bfloat16),
        pairs_in[:, :hf_rows].astype(jnp.bfloat16),
        band_blocks,
        long_read,
        targets_read,
    )
    hidden_sum = both_sum[:h_rows].reshape(h_rows, nodes)
    feat_sum = both_sum[h_rows:].reshape(f_rows, nodes)

    landing = (
        landing_blocks.reshape(-1)[:, None] == jnp.arange(NB, dtype=jnp.int32)[None, :]
    ).astype(jnp.float32)
    sg_sum = (
        sg_middle
        + jnp.concatenate([sg_prior[:, 1:], arrived[down][2, hf_rows:][:, None]], 1)
        + jnp.concatenate([arrived[up][2, hf_rows:][:, None], sg_later[:, :-1]], 1)
        + jnp.einsum("kb,kfm->fbm", landing, pairs_in[:, hf_rows:], precision=HI)
    )
    class_back = sg_sum.reshape(c_rows, nodes).astype(jnp.bfloat16)

    hidden_act = jax.nn.silu(hidden_sum).astype(jnp.bfloat16)

    my_rows = lax.dynamic_slice_in_dim(weight_out, col_index * hidden_count, hidden_count, 0)
    class_part = jnp.einsum("hc,hn->cn", my_rows, hidden_act, preferred_element_type=jnp.float32)
    part_blocks = class_part.reshape(col_devices, c_rows, nodes)
    mine = jnp.broadcast_to(class_back.astype(jnp.float32)[None], part_blocks.shape)
    outgoing = jnp.stack([part_blocks, mine], 1)
    incoming = lax.all_to_all(outgoing, "col", 0, 0, tiled=True)
    class_in = jnp.sum(incoming[:, 0], axis=0).astype(jnp.bfloat16)
    all_back = incoming[:, 1].astype(jnp.bfloat16).reshape(col_devices * c_rows, nodes)

    hidden_back = jnp.einsum("hc,cn->hn", my_rows, all_back, preferred_element_type=jnp.float32)
    second_part = jnp.einsum("hn,cn->hc", hidden_act, all_back, preferred_element_type=jnp.float32)

    sigmoid_val = jax.nn.sigmoid(hidden_sum)
    slope_back = (hidden_back * sigmoid_val * (1.0 + hidden_sum * (1.0 - sigmoid_val))).astype(
        jnp.bfloat16
    )
    first_part = jnp.einsum(
        "in,hn->ih", feat_sum, slope_back.astype(jnp.float32), precision=HI
    )

    flat = jnp.concatenate([first_part.reshape(-1), second_part.reshape(-1)])
    pieces = lax.all_to_all(flat.reshape(row_devices, -1), "row", 0, 0, tiled=True)
    class_blocks = class_in.reshape(c_rows, NB, BLK)
    class_pick = jnp.take(class_blocks.transpose(1, 0, 2), pick, axis=0)
    class_pick = class_pick.reshape(len(shifts()), 3, c_rows, BLK)
    class_pick, pieces = lax.optimization_barrier((class_pick, pieces))
    class_arrived = [send_by(class_pick[i], "row", e) for i, e in enumerate(shifts())]
    class_pairs = jnp.concatenate([a[:2] for a in class_arrived], 0)
    scores = forward_sum(
        class_blocks,
        class_arrived[up][2],
        class_arrived[down][2],
        class_pairs,
        band_blocks,
        long_read,
        targets_read,
    ).reshape(c_rows, nodes).astype(jnp.bfloat16)

    summed = jnp.sum(pieces, axis=0, keepdims=True)
    spread = jnp.broadcast_to(summed, (row_devices, summed.shape[1]))
    flat = lax.all_to_all(spread, "row", 0, 0, tiled=True).reshape(-1)
    first_grad = flat[: first_part.size].reshape(first_part.shape)
    second_grad = flat[first_part.size:].reshape(second_part.shape)
    return (scores, first_grad, second_grad)


def solution(mesh):
    return jax.shard_map(
        local,
        mesh=mesh,
        in_specs=(
            P(None, "row"),
            P(None, "col"),
            P(),
            P("col", "row"),
            P("row", None, None, None),
            P("row", None, None),
            P("row", None),
            P(),
            P(),
        ),
        out_specs=(P("col", "row"), P(None, "col"), P("col", None)),
        check_vma=False,
    )
```

```python
import jax
import jax.numpy as jnp
from jax import lax
from jax.sharding import PartitionSpec as P

BLK = 128
NB = 16
REACH = 3
SLOTS = 12
HI = lax.Precision.HIGHEST


def shifts():
    return [e for e in range(-REACH, REACH + 1) if e != 0]


def shift_index(e):
    return e + REACH if e < 0 else e + REACH - 1


def send_by(x, axis, by):
    devices = lax.axis_size(axis)
    return lax.ppermute(x, axis, [(i, (i + by) % devices) for i in range(devices)])


def swap_with(x, axis, mask):
    devices = lax.axis_size(axis)
    return lax.ppermute(x, axis, [(i, i ^ mask) for i in range(devices)])


def slot_tables(long_sources, me, row_devices):
    steps = jnp.array(shifts(), jnp.int32)
    partners = jnp.concatenate([jnp.mod(me + steps, row_devices), jnp.mod(me - steps, row_devices)])
    rows = jnp.take(long_sources, partners, axis=0)
    hit = (rows // NB) == me
    earlier = jnp.arange(SLOTS)[None, :] < jnp.arange(SLOTS)[:, None]
    rank = jnp.sum((hit[:, None, :] & earlier[None]).astype(jnp.int32), axis=2)
    local = rows % NB
    picks = [jnp.sum(jnp.where(hit & (rank == q), local, 0), axis=1) for q in range(2)]
    table = jnp.stack(picks, 1)
    return table[: len(shifts())], table[len(shifts()):]


def own_slot_pairs(long_sources, me, row_devices):
    source = lax.dynamic_index_in_dim(long_sources, me, 0, keepdims=False)
    owner = source // NB
    offset = jnp.mod(owner - me, row_devices)
    offset = jnp.where(offset > row_devices // 2, offset - row_devices, offset)
    same = (owner[:, None] == owner[None, :]) & (
        jnp.arange(SLOTS)[None, :] < jnp.arange(SLOTS)[:, None]
    )
    rank = jnp.sum(same.astype(jnp.int32), axis=1)
    send_position = jnp.where(offset < 0, offset + REACH, offset + REACH - 1)
    read_position = jnp.where(offset > 0, -offset + REACH, -offset + REACH - 1)
    return send_position * 2 + rank, read_position * 2 + rank


def inverse_of(pairs):
    return jnp.sum(
        jnp.where(pairs[None, :] == jnp.arange(SLOTS)[:, None], jnp.arange(SLOTS)[None, :], 0), axis=1
    )


def forward_sum(blocks, prev_edge, next_edge, panels, band_blocks, long_in_order, targets_in_order):
    earlier = jnp.concatenate([prev_edge[:, None], blocks[:, :-1]], 1)
    onward = jnp.concatenate([blocks[:, 1:], next_edge[:, None]], 1)
    near = jnp.einsum("fbm,bnm->fbn", earlier, band_blocks[:, 0], preferred_element_type=jnp.float32)
    near = near + jnp.einsum("fbm,bnm->fbn", blocks, band_blocks[:, 1], preferred_element_type=jnp.float32)
    near = near + jnp.einsum("fbm,bnm->fbn", onward, band_blocks[:, 2], preferred_element_type=jnp.float32)
    contrib = jnp.einsum("kfm,knm->kfn", panels, long_in_order, preferred_element_type=jnp.float32)
    far = jnp.einsum("kb,kfn->fbn", targets_in_order, contrib, precision=HI)
    return near + far


def local(
    features,
    weight_in,
    weight_out,
    score_grad,
    band_blocks,
    long_blocks,
    long_rows,
    long_sources,
    long_counts,
):
    row_devices = lax.axis_size("row")
    col_devices = lax.axis_size("col")
    me = lax.axis_index("row")
    col_index = lax.axis_index("col")
    row_ids = long_rows[0]
    hidden_count = weight_in.shape[1]
    class_count = score_grad.shape[0]
    nodes = features.shape[1]
    h_rows = hidden_count
    f_rows = features.shape[0]
    c_rows = class_count
    hf_rows = h_rows + f_rows
    up = shift_index(1)
    down = shift_index(-1)

    live_count = lax.dynamic_index_in_dim(long_counts, me, 0, keepdims=False)
    is_live = jnp.arange(SLOTS, dtype=jnp.int32) < live_count
    live = is_live.astype(jnp.float32)
    targets = (
        (row_ids[:, None] == jnp.arange(NB, dtype=jnp.int32)[None, :]) & is_live[:, None]
    ).astype(jnp.float32)
    send_pair, read_pair = own_slot_pairs(long_sources, me, row_devices)
    sending_slot = inverse_of(send_pair)
    reading_slot = inverse_of(read_pair)
    long_read = jnp.take(long_blocks, reading_slot, axis=0)
    targets_read = jnp.take(targets, reading_slot, axis=0)
    wanted, landing_blocks = slot_tables(long_sources, me, row_devices)
    edge_block = jnp.array([[NB - 1 if e == 1 else 0] for e in shifts()], jnp.int32)
    pick = jnp.concatenate([wanted, edge_block], 1).reshape(-1)

    hidden_in = jnp.einsum(
        "ih,in->hn", weight_in, features, preferred_element_type=jnp.float32
    ).astype(jnp.bfloat16)
    both_in = jnp.concatenate([hidden_in, features], 0)
    both_blocks = both_in.reshape(hf_rows, NB, BLK)

    sg_blocks = score_grad.reshape(class_count, NB, BLK)
    sg_prior = jnp.einsum("fbn,bnm->fbm", sg_blocks, band_blocks[:, 0], preferred_element_type=jnp.float32)
    sg_middle = jnp.einsum("fbn,bnm->fbm", sg_blocks, band_blocks[:, 1], preferred_element_type=jnp.float32)
    sg_later = jnp.einsum("fbn,bnm->fbm", sg_blocks, band_blocks[:, 2], preferred_element_type=jnp.float32)
    sg_rows = jnp.take(sg_blocks, jnp.take(row_ids, sending_slot), axis=1)
    sg_out = jnp.einsum(
        "fkn,knm->kfm", sg_rows, jnp.take(long_blocks, sending_slot, axis=0),
        preferred_element_type=jnp.float32,
    )
    sg_out = sg_out * jnp.take(live, sending_slot)[:, None, None]
    sg_edges = jnp.zeros((len(shifts()), 1, c_rows, BLK), jnp.float32)
    sg_edges = sg_edges.at[up, 0].set(sg_later[:, NB - 1]).at[down, 0].set(sg_prior[:, 0])
    sg_send = jnp.concatenate([sg_out.reshape(len(shifts()), 2, c_rows, BLK), sg_edges], 1)

    picked = jnp.take(both_blocks.transpose(1, 0, 2), pick, axis=0)
    picked = picked.reshape(len(shifts()), 3, hf_rows, BLK)
    sg_high = sg_send.astype(jnp.bfloat16)
    sg_low = (sg_send - sg_high.astype(jnp.float32)).astype(jnp.bfloat16)
    send_all = jnp.concatenate([picked, sg_high, sg_low], 2)
    arrived = [send_by(send_all[i], "row", e) for i, e in enumerate(shifts())]
    arrived = [
        (a[:, :hf_rows], a[:, hf_rows:hf_rows + c_rows].astype(jnp.float32)
         + a[:, hf_rows + c_rows:].astype(jnp.float32))
        for a in arrived
    ]
    pairs_in = jnp.concatenate([a[0][:2] for a in arrived], 0)
    sg_pairs = jnp.concatenate([a[1][:2] for a in arrived], 0)

    both_sum = forward_sum(
        both_blocks,
        arrived[up][0][2],
        arrived[down][0][2],
        pairs_in,
        band_blocks,
        long_read,
        targets_read,
    )
    hidden_sum = both_sum[:h_rows].reshape(h_rows, nodes)
    feat_sum = both_sum[h_rows:].reshape(f_rows, nodes)

    landing = (
        landing_blocks.reshape(-1)[:, None] == jnp.arange(NB, dtype=jnp.int32)[None, :]
    ).astype(jnp.float32)
    sg_sum = (
        sg_middle
        + jnp.concatenate([sg_prior[:, 1:], arrived[down][1][2][:, None]], 1)
        + jnp.concatenate([arrived[up][1][2][:, None], sg_later[:, :-1]], 1)
        + jnp.einsum("kb,kfm->fbm", landing, sg_pairs, precision=HI)
    )
    class_back = sg_sum.reshape(c_rows, nodes).astype(jnp.bfloat16)

    hidden_act = jax.nn.silu(hidden_sum).astype(jnp.bfloat16)

    my_rows = lax.dynamic_slice_in_dim(weight_out, col_index * hidden_count, hidden_count, 0)
    class_part = jnp.einsum("hc,hn->cn", my_rows, hidden_act, preferred_element_type=jnp.float32)
    part_blocks = class_part.reshape(col_devices, c_rows, nodes)
    mine = jnp.broadcast_to(class_back.astype(jnp.float32)[None], part_blocks.shape)
    outgoing = jnp.stack([part_blocks, mine], 1)
    incoming = lax.all_to_all(outgoing, "col", 0, 0, tiled=True)
    class_in = jnp.sum(incoming[:, 0], axis=0).astype(jnp.bfloat16)
    all_back = incoming[:, 1].astype(jnp.bfloat16).reshape(col_devices * c_rows, nodes)

    hidden_back = jnp.einsum("hc,cn->hn", my_rows, all_back, preferred_element_type=jnp.float32)
    second_part = jnp.einsum("hn,cn->hc", hidden_act, all_back, preferred_element_type=jnp.float32)

    sigmoid_val = jax.nn.sigmoid(hidden_sum)
    slope_back = (hidden_back * sigmoid_val * (1.0 + hidden_sum * (1.0 - sigmoid_val))).astype(
        jnp.bfloat16
    )
    first_part = jnp.einsum(
        "in,hn->ih", feat_sum, slope_back.astype(jnp.float32), precision=HI
    )

    flat = jnp.concatenate([first_part.reshape(-1), second_part.reshape(-1)])
    pieces = lax.all_to_all(flat.reshape(row_devices, -1), "row", 0, 0, tiled=True)
    class_blocks = class_in.reshape(c_rows, NB, BLK)
    class_pick = jnp.take(class_blocks.transpose(1, 0, 2), pick, axis=0)
    class_pick = class_pick.reshape(len(shifts()), 3, c_rows, BLK)
    class_pick, pieces = lax.optimization_barrier((class_pick, pieces))
    class_arrived = [send_by(class_pick[i], "row", e) for i, e in enumerate(shifts())]
    class_pairs = jnp.concatenate([a[:2] for a in class_arrived], 0)
    scores = forward_sum(
        class_blocks,
        class_arrived[up][2],
        class_arrived[down][2],
        class_pairs,
        band_blocks,
        long_read,
        targets_read,
    ).reshape(c_rows, nodes).astype(jnp.bfloat16)

    summed = jnp.sum(pieces, axis=0, keepdims=True)
    spread = jnp.broadcast_to(summed, (row_devices, summed.shape[1]))
    flat = lax.all_to_all(spread, "row", 0, 0, tiled=True).reshape(-1)
    first_grad = flat[: first_part.size].reshape(first_part.shape)
    second_grad = flat[first_part.size:].reshape(second_part.shape)
    return (scores, first_grad, second_grad)


def solution(mesh):
    return jax.shard_map(
        local,
        mesh=mesh,
        in_specs=(
            P(None, "row"),
            P(None, "col"),
            P(),
            P("col", "row"),
            P("row", None, None, None),
            P("row", None, None),
            P("row", None),
            P(),
            P(),
        ),
        out_specs=(P("col", "row"), P(None, "col"), P("col", None)),
        check_vma=False,
    )
```

```python
import jax
import jax.numpy as jnp
from jax import lax
from jax.sharding import PartitionSpec as P

BLK = 128
NB = 16
REACH = 3
SLOTS = 12
HI = lax.Precision.HIGHEST


def shifts():
    return [e for e in range(-REACH, REACH + 1) if e != 0]


def shift_index(e):
    return e + REACH if e < 0 else e + REACH - 1


def send_by(x, axis, by):
    devices = lax.axis_size(axis)
    return lax.ppermute(x, axis, [(i, (i + by) % devices) for i in range(devices)])


def swap_with(x, axis, mask):
    devices = lax.axis_size(axis)
    return lax.ppermute(x, axis, [(i, i ^ mask) for i in range(devices)])


def slot_tables(long_sources, me, row_devices):
    steps = jnp.array(shifts(), jnp.int32)
    partners = jnp.concatenate([jnp.mod(me + steps, row_devices), jnp.mod(me - steps, row_devices)])
    rows = jnp.take(long_sources, partners, axis=0)
    hit = (rows // NB) == me
    earlier = jnp.arange(SLOTS)[None, :] < jnp.arange(SLOTS)[:, None]
    rank = jnp.sum((hit[:, None, :] & earlier[None]).astype(jnp.int32), axis=2)
    local = rows % NB
    picks = [jnp.sum(jnp.where(hit & (rank == q), local, 0), axis=1) for q in range(2)]
    table = jnp.stack(picks, 1)
    return table[: len(shifts())], table[len(shifts()):]


def own_slot_pairs(long_sources, me, row_devices):
    source = lax.dynamic_index_in_dim(long_sources, me, 0, keepdims=False)
    owner = source // NB
    offset = jnp.mod(owner - me, row_devices)
    offset = jnp.where(offset > row_devices // 2, offset - row_devices, offset)
    same = (owner[:, None] == owner[None, :]) & (
        jnp.arange(SLOTS)[None, :] < jnp.arange(SLOTS)[:, None]
    )
    rank = jnp.sum(same.astype(jnp.int32), axis=1)
    send_position = jnp.where(offset < 0, offset + REACH, offset + REACH - 1)
    read_position = jnp.where(offset > 0, -offset + REACH, -offset + REACH - 1)
    return send_position * 2 + rank, read_position * 2 + rank


def inverse_of(pairs):
    return jnp.sum(
        jnp.where(pairs[None, :] == jnp.arange(SLOTS)[:, None], jnp.arange(SLOTS)[None, :], 0), axis=1
    )


def forward_sum(blocks, prev_edge, next_edge, panels, band_blocks, long_in_order, targets_in_order):
    earlier = jnp.concatenate([prev_edge[:, None], blocks[:, :-1]], 1)
    onward = jnp.concatenate([blocks[:, 1:], next_edge[:, None]], 1)
    near = jnp.einsum("fbm,bnm->fbn", earlier, band_blocks[:, 0], preferred_element_type=jnp.float32)
    near = near + jnp.einsum("fbm,bnm->fbn", blocks, band_blocks[:, 1], preferred_element_type=jnp.float32)
    near = near + jnp.einsum("fbm,bnm->fbn", onward, band_blocks[:, 2], preferred_element_type=jnp.float32)
    contrib = jnp.einsum("kfm,knm->kfn", panels, long_in_order, preferred_element_type=jnp.float32)
    far = jnp.einsum("kb,kfn->fbn", targets_in_order, contrib, precision=HI)
    return near + far


def local(
    features,
    weight_in,
    weight_out,
    score_grad,
    band_blocks,
    long_blocks,
    long_rows,
    long_sources,
    long_counts,
):
    row_devices = lax.axis_size("row")
    col_devices = lax.axis_size("col")
    me = lax.axis_index("row")
    col_index = lax.axis_index("col")
    row_ids = long_rows[0]
    hidden_count = weight_in.shape[1]
    class_count = score_grad.shape[0]
    nodes = features.shape[1]
    h_rows = hidden_count
    f_rows = features.shape[0]
    c_rows = class_count
    hf_rows = h_rows + f_rows
    up = shift_index(1)
    down = shift_index(-1)

    live_count = lax.dynamic_index_in_dim(long_counts, me, 0, keepdims=False)
    is_live = jnp.arange(SLOTS, dtype=jnp.int32) < live_count
    live = is_live.astype(jnp.float32)
    targets = (
        (row_ids[:, None] == jnp.arange(NB, dtype=jnp.int32)[None, :]) & is_live[:, None]
    ).astype(jnp.float32)
    send_pair, read_pair = own_slot_pairs(long_sources, me, row_devices)
    sending_slot = inverse_of(send_pair)
    reading_slot = inverse_of(read_pair)
    long_read = jnp.take(long_blocks, reading_slot, axis=0)
    targets_read = jnp.take(targets, reading_slot, axis=0)
    wanted, landing_blocks = slot_tables(long_sources, me, row_devices)
    edge_block = jnp.array([[NB - 1 if e == 1 else 0] for e in shifts()], jnp.int32)
    pick = jnp.concatenate([wanted, edge_block], 1).reshape(-1)

    hidden_in = jnp.einsum(
        "ih,in->hn", weight_in, features, preferred_element_type=jnp.float32
    ).astype(jnp.bfloat16)
    both_in = jnp.concatenate([hidden_in, features], 0)
    both_blocks = both_in.reshape(hf_rows, NB, BLK)

    sg_blocks = score_grad.reshape(class_count, NB, BLK)
    sg_prior = jnp.einsum("fbn,bnm->fbm", sg_blocks, band_blocks[:, 0], preferred_element_type=jnp.float32)
    sg_middle = jnp.einsum("fbn,bnm->fbm", sg_blocks, band_blocks[:, 1], preferred_element_type=jnp.float32)
    sg_later = jnp.einsum("fbn,bnm->fbm", sg_blocks, band_blocks[:, 2], preferred_element_type=jnp.float32)
    sg_rows = jnp.take(sg_blocks, jnp.take(row_ids, sending_slot), axis=1)
    sg_out = jnp.einsum(
        "fkn,knm->kfm", sg_rows, jnp.take(long_blocks, sending_slot, axis=0),
        preferred_element_type=jnp.float32,
    )
    sg_out = sg_out * jnp.take(live, sending_slot)[:, None, None]
    sg_edges = jnp.zeros((len(shifts()), 1, c_rows, BLK), jnp.float32)
    sg_edges = sg_edges.at[up, 0].set(sg_later[:, NB - 1]).at[down, 0].set(sg_prior[:, 0])
    sg_send = jnp.concatenate([sg_out.reshape(len(shifts()), 2, c_rows, BLK), sg_edges], 1)

    picked = jnp.take(both_blocks.transpose(1, 0, 2), pick, axis=0)
    picked = picked.reshape(len(shifts()), 3, hf_rows, BLK).astype(jnp.float32)
    send_all = jnp.concatenate([picked, sg_send], 2)
    arrived = [send_by(send_all[i], "row", e) for i, e in enumerate(shifts())]
    pairs_in = jnp.concatenate([a[:2] for a in arrived], 0)

    hidden_sum = forward_sum(
        both_blocks[:h_rows],
        arrived[up][2, :h_rows].astype(jnp.bfloat16),
        arrived[down][2, :h_rows].astype(jnp.bfloat16),
        pairs_in[:, :h_rows].astype(jnp.bfloat16),
        band_blocks,
        long_read,
        targets_read,
    ).reshape(h_rows, nodes)
    feat_sum = forward_sum(
        both_blocks[h_rows:],
        arrived[up][2, h_rows:hf_rows].astype(jnp.bfloat16),
        arrived[down][2, h_rows:hf_rows].astype(jnp.bfloat16),
        pairs_in[:, h_rows:hf_rows].astype(jnp.bfloat16),
        band_blocks,
        long_read,
        targets_read,
    ).reshape(f_rows, nodes)

    landing = (
        landing_blocks.reshape(-1)[:, None] == jnp.arange(NB, dtype=jnp.int32)[None, :]
    ).astype(jnp.float32)
    sg_sum = (
        sg_middle
        + jnp.concatenate([sg_prior[:, 1:], arrived[down][2, hf_rows:][:, None]], 1)
        + jnp.concatenate([arrived[up][2, hf_rows:][:, None], sg_later[:, :-1]], 1)
        + jnp.einsum("kb,kfm->fbm", landing, pairs_in[:, hf_rows:], precision=HI)
    )
    class_back = sg_sum.reshape(c_rows, nodes).astype(jnp.bfloat16)

    hidden_act = jax.nn.silu(hidden_sum).astype(jnp.bfloat16)

    my_rows = lax.dynamic_slice_in_dim(weight_out, col_index * hidden_count, hidden_count, 0)
    class_part = jnp.einsum("hc,hn->cn", my_rows, hidden_act, preferred_element_type=jnp.float32)
    part_blocks = class_part.reshape(col_devices, c_rows, nodes)
    mine = jnp.broadcast_to(class_back.astype(jnp.float32)[None], part_blocks.shape)
    outgoing = jnp.stack([part_blocks, mine], 1)
    incoming = lax.all_to_all(outgoing, "col", 0, 0, tiled=True)
    class_in = jnp.sum(incoming[:, 0], axis=0).astype(jnp.bfloat16)
    all_back = incoming[:, 1].astype(jnp.bfloat16).reshape(col_devices * c_rows, nodes)

    hidden_back = jnp.einsum("hc,cn->hn", my_rows, all_back, preferred_element_type=jnp.float32)
    second_part = jnp.einsum("hn,cn->hc", hidden_act, all_back, preferred_element_type=jnp.float32)

    sigmoid_val = jax.nn.sigmoid(hidden_sum)
    slope_back = (hidden_back * sigmoid_val * (1.0 + hidden_sum * (1.0 - sigmoid_val))).astype(
        jnp.bfloat16
    )
    first_part = jnp.einsum(
        "in,hn->ih", feat_sum, slope_back.astype(jnp.float32), precision=HI
    )

    flat = jnp.concatenate([first_part.reshape(-1), second_part.reshape(-1)])
    pieces = lax.all_to_all(flat.reshape(row_devices, -1), "row", 0, 0, tiled=True)
    class_blocks = class_in.reshape(c_rows, NB, BLK)
    class_pick = jnp.take(class_blocks.transpose(1, 0, 2), pick, axis=0)
    class_pick = class_pick.reshape(len(shifts()), 3, c_rows, BLK)
    class_pick, pieces = lax.optimization_barrier((class_pick, pieces))
    class_arrived = [send_by(class_pick[i], "row", e) for i, e in enumerate(shifts())]
    class_pairs = jnp.concatenate([a[:2] for a in class_arrived], 0)
    scores = forward_sum(
        class_blocks,
        class_arrived[up][2],
        class_arrived[down][2],
        class_pairs,
        band_blocks,
        long_read,
        targets_read,
    ).reshape(c_rows, nodes).astype(jnp.bfloat16)

    summed = jnp.sum(pieces, axis=0, keepdims=True)
    spread = jnp.broadcast_to(summed, (row_devices, summed.shape[1]))
    flat = lax.all_to_all(spread, "row", 0, 0, tiled=True).reshape(-1)
    first_grad = flat[: first_part.size].reshape(first_part.shape)
    second_grad = flat[first_part.size:].reshape(second_part.shape)
    return (scores, first_grad, second_grad)


def solution(mesh):
    return jax.shard_map(
        local,
        mesh=mesh,
        in_specs=(
            P(None, "row"),
            P(None, "col"),
            P(),
            P("col", "row"),
            P("row", None, None, None),
            P("row", None, None),
            P("row", None),
            P(),
            P(),
        ),
        out_specs=(P("col", "row"), P(None, "col"), P("col", None)),
        check_vma=False,
    )
```

```python
import jax
import jax.numpy as jnp
from jax import lax
from jax.sharding import PartitionSpec as P

BLK = 128
NB = 16
REACH = 3
SLOTS = 12
HI = lax.Precision.HIGHEST


def shifts():
    return [e for e in range(-REACH, REACH + 1) if e != 0]


def shift_index(e):
    return e + REACH if e < 0 else e + REACH - 1


def send_by(x, axis, by):
    devices = lax.axis_size(axis)
    return lax.ppermute(x, axis, [(i, (i + by) % devices) for i in range(devices)])


def swap_with(x, axis, mask):
    devices = lax.axis_size(axis)
    return lax.ppermute(x, axis, [(i, i ^ mask) for i in range(devices)])


def slot_tables(long_sources, me, row_devices):
    steps = jnp.array(shifts(), jnp.int32)
    partners = jnp.concatenate([jnp.mod(me + steps, row_devices), jnp.mod(me - steps, row_devices)])
    rows = jnp.take(long_sources, partners, axis=0)
    hit = (rows // NB) == me
    earlier = jnp.arange(SLOTS)[None, :] < jnp.arange(SLOTS)[:, None]
    rank = jnp.sum((hit[:, None, :] & earlier[None]).astype(jnp.int32), axis=2)
    local = rows % NB
    picks = [jnp.sum(jnp.where(hit & (rank == q), local, 0), axis=1) for q in range(2)]
    table = jnp.stack(picks, 1)
    return table[: len(shifts())], table[len(shifts()):]


def own_slot_pairs(long_sources, me, row_devices):
    source = lax.dynamic_index_in_dim(long_sources, me, 0, keepdims=False)
    owner = source // NB
    offset = jnp.mod(owner - me, row_devices)
    offset = jnp.where(offset > row_devices // 2, offset - row_devices, offset)
    same = (owner[:, None] == owner[None, :]) & (
        jnp.arange(SLOTS)[None, :] < jnp.arange(SLOTS)[:, None]
    )
    rank = jnp.sum(same.astype(jnp.int32), axis=1)
    send_position = jnp.where(offset < 0, offset + REACH, offset + REACH - 1)
    read_position = jnp.where(offset > 0, -offset + REACH, -offset + REACH - 1)
    return send_position * 2 + rank, read_position * 2 + rank


def inverse_of(pairs):
    return jnp.sum(
        jnp.where(pairs[None, :] == jnp.arange(SLOTS)[:, None], jnp.arange(SLOTS)[None, :], 0), axis=1
    )


def forward_sum(blocks, prev_edge, next_edge, panels, band_blocks, long_in_order, targets_in_order):
    earlier = jnp.concatenate([prev_edge[:, None], blocks[:, :-1]], 1)
    onward = jnp.concatenate([blocks[:, 1:], next_edge[:, None]], 1)
    near = jnp.einsum("fbm,bnm->fbn", earlier, band_blocks[:, 0], preferred_element_type=jnp.float32)
    near = near + jnp.einsum("fbm,bnm->fbn", blocks, band_blocks[:, 1], preferred_element_type=jnp.float32)
    near = near + jnp.einsum("fbm,bnm->fbn", onward, band_blocks[:, 2], preferred_element_type=jnp.float32)
    contrib = jnp.einsum("kfm,knm->kfn", panels, long_in_order, preferred_element_type=jnp.float32)
    far = jnp.einsum("kb,kfn->fbn", targets_in_order, contrib, precision=HI)
    return near + far


def local(
    features,
    weight_in,
    weight_out,
    score_grad,
    band_blocks,
    long_blocks,
    long_rows,
    long_sources,
    long_counts,
):
    row_devices = lax.axis_size("row")
    col_devices = lax.axis_size("col")
    me = lax.axis_index("row")
    col_index = lax.axis_index("col")
    row_ids = long_rows[0]
    hidden_count = weight_in.shape[1]
    class_count = score_grad.shape[0]
    nodes = features.shape[1]
    h_rows = hidden_count
    f_rows = features.shape[0]
    c_rows = class_count
    hf_rows = h_rows + f_rows
    up = shift_index(1)
    down = shift_index(-1)

    live_count = lax.dynamic_index_in_dim(long_counts, me, 0, keepdims=False)
    is_live = jnp.arange(SLOTS, dtype=jnp.int32) < live_count
    live = is_live.astype(jnp.float32)
    targets = (
        (row_ids[:, None] == jnp.arange(NB, dtype=jnp.int32)[None, :]) & is_live[:, None]
    ).astype(jnp.float32)
    send_pair, read_pair = own_slot_pairs(long_sources, me, row_devices)
    sending_slot = inverse_of(send_pair)
    reading_slot = inverse_of(read_pair)
    long_read = jnp.take(long_blocks, reading_slot, axis=0)
    targets_read = jnp.take(targets, reading_slot, axis=0)
    wanted, landing_blocks = slot_tables(long_sources, me, row_devices)
    edge_block = jnp.array([[NB - 1 if e == 1 else 0] for e in shifts()], jnp.int32)
    pick = jnp.concatenate([wanted, edge_block], 1).reshape(-1)

    hidden_in = jnp.einsum(
        "ih,in->hn", weight_in, features, preferred_element_type=jnp.float32
    ).astype(jnp.bfloat16)
    both_in = jnp.concatenate([hidden_in, features], 0)
    both_blocks = both_in.reshape(hf_rows, NB, BLK)

    sg_blocks = score_grad.reshape(class_count, NB, BLK)
    sg_prior = jnp.einsum("fbn,bnm->fbm", sg_blocks, band_blocks[:, 0], preferred_element_type=jnp.float32)
    sg_middle = jnp.einsum("fbn,bnm->fbm", sg_blocks, band_blocks[:, 1], preferred_element_type=jnp.float32)
    sg_later = jnp.einsum("fbn,bnm->fbm", sg_blocks, band_blocks[:, 2], preferred_element_type=jnp.float32)
    sg_rows = jnp.take(sg_blocks, jnp.take(row_ids, sending_slot), axis=1)
    sg_out = jnp.einsum(
        "fkn,knm->kfm", sg_rows, jnp.take(long_blocks, sending_slot, axis=0),
        preferred_element_type=jnp.float32,
    )
    sg_out = sg_out * jnp.take(live, sending_slot)[:, None, None]
    edge_later = jnp.dot(sg_blocks[:, NB - 1], band_blocks[NB - 1, 2], preferred_element_type=jnp.float32)
    edge_prior = jnp.dot(sg_blocks[:, 0], band_blocks[0, 0], preferred_element_type=jnp.float32)
    no_edge = jnp.zeros((c_rows, BLK), jnp.float32)
    sg_edges = jnp.stack(
        [edge_later if e == 1 else edge_prior if e == -1 else no_edge for e in shifts()], 0
    )[:, None]
    sg_send = jnp.concatenate([sg_out.reshape(len(shifts()), 2, c_rows, BLK), sg_edges], 1)

    picked = jnp.take(both_blocks.transpose(1, 0, 2), pick, axis=0)
    picked = picked.reshape(len(shifts()), 3, hf_rows, BLK).astype(jnp.float32)
    send_all = jnp.concatenate([picked, sg_send], 2)
    arrived = [send_by(send_all[i], "row", e) for i, e in enumerate(shifts())]
    pairs_in = jnp.concatenate([a[:2] for a in arrived], 0)

    both_sum = forward_sum(
        both_blocks,
        arrived[up][2, :hf_rows].astype(jnp.bfloat16),
        arrived[down][2, :hf_rows].astype(jnp.bfloat16),
        pairs_in[:, :hf_rows].astype(jnp.bfloat16),
        band_blocks,
        long_read,
        targets_read,
    )
    hidden_sum = both_sum[:h_rows].reshape(h_rows, nodes)
    feat_sum = both_sum[h_rows:].reshape(f_rows, nodes)

    landing = (
        landing_blocks.reshape(-1)[:, None] == jnp.arange(NB, dtype=jnp.int32)[None, :]
    ).astype(jnp.float32)
    sg_sum = (
        sg_middle
        + jnp.concatenate([sg_prior[:, 1:], arrived[down][2, hf_rows:][:, None]], 1)
        + jnp.concatenate([arrived[up][2, hf_rows:][:, None], sg_later[:, :-1]], 1)
        + jnp.einsum("kb,kfm->fbm", landing, pairs_in[:, hf_rows:], precision=HI)
    )
    class_back = sg_sum.reshape(c_rows, nodes).astype(jnp.bfloat16)

    hidden_act = jax.nn.silu(hidden_sum).astype(jnp.bfloat16)

    my_rows = lax.dynamic_slice_in_dim(weight_out, col_index * hidden_count, hidden_count, 0)
    class_part = jnp.einsum("hc,hn->cn", my_rows, hidden_act, preferred_element_type=jnp.float32)
    part_blocks = class_part.reshape(col_devices, c_rows, nodes)
    mine = jnp.broadcast_to(class_back.astype(jnp.float32)[None], part_blocks.shape)
    outgoing = jnp.stack([part_blocks, mine], 1)
    incoming = lax.all_to_all(outgoing, "col", 0, 0, tiled=True)
    class_in = jnp.sum(incoming[:, 0], axis=0).astype(jnp.bfloat16)
    all_back = incoming[:, 1].astype(jnp.bfloat16).reshape(col_devices * c_rows, nodes)

    hidden_back = jnp.einsum("hc,cn->hn", my_rows, all_back, preferred_element_type=jnp.float32)
    second_part = jnp.einsum("hn,cn->hc", hidden_act, all_back, preferred_element_type=jnp.float32)

    sigmoid_val = jax.nn.sigmoid(hidden_sum)
    slope_back = (hidden_back * sigmoid_val * (1.0 + hidden_sum * (1.0 - sigmoid_val))).astype(
        jnp.bfloat16
    )
    first_part = jnp.einsum(
        "in,hn->ih", feat_sum, slope_back.astype(jnp.float32), precision=HI
    )

    flat = jnp.concatenate([first_part.reshape(-1), second_part.reshape(-1)])
    pieces = lax.all_to_all(flat.reshape(row_devices, -1), "row", 0, 0, tiled=True)
    class_blocks = class_in.reshape(c_rows, NB, BLK)
    class_pick = jnp.take(class_blocks.transpose(1, 0, 2), pick, axis=0)
    class_pick = class_pick.reshape(len(shifts()), 3, c_rows, BLK)
    class_pick, pieces = lax.optimization_barrier((class_pick, pieces))
    class_arrived = [send_by(class_pick[i], "row", e) for i, e in enumerate(shifts())]
    class_pairs = jnp.concatenate([a[:2] for a in class_arrived], 0)
    scores = forward_sum(
        class_blocks,
        class_arrived[up][2],
        class_arrived[down][2],
        class_pairs,
        band_blocks,
        long_read,
        targets_read,
    ).reshape(c_rows, nodes).astype(jnp.bfloat16)

    summed = jnp.sum(pieces, axis=0, keepdims=True)
    spread = jnp.broadcast_to(summed, (row_devices, summed.shape[1]))
    flat = lax.all_to_all(spread, "row", 0, 0, tiled=True).reshape(-1)
    first_grad = flat[: first_part.size].reshape(first_part.shape)
    second_grad = flat[first_part.size:].reshape(second_part.shape)
    return (scores, first_grad, second_grad)


def solution(mesh):
    return jax.shard_map(
        local,
        mesh=mesh,
        in_specs=(
            P(None, "row"),
            P(None, "col"),
            P(),
            P("col", "row"),
            P("row", None, None, None),
            P("row", None, None),
            P("row", None),
            P(),
            P(),
        ),
        out_specs=(P("col", "row"), P(None, "col"), P("col", None)),
        check_vma=False,
    )
```

```python
import jax
import jax.numpy as jnp
from jax import lax
from jax.sharding import PartitionSpec as P

BLK = 128
NB = 16
REACH = 3
SLOTS = 12
HI = lax.Precision.HIGHEST


def shifts():
    return [e for e in range(-REACH, REACH + 1) if e != 0]


def shift_index(e):
    return e + REACH if e < 0 else e + REACH - 1


def send_by(x, axis, by):
    devices = lax.axis_size(axis)
    return lax.ppermute(x, axis, [(i, (i + by) % devices) for i in range(devices)])


def swap_with(x, axis, mask):
    devices = lax.axis_size(axis)
    return lax.ppermute(x, axis, [(i, i ^ mask) for i in range(devices)])


def slot_tables(long_sources, me, row_devices):
    steps = jnp.array(shifts(), jnp.int32)
    partners = jnp.concatenate([jnp.mod(me + steps, row_devices), jnp.mod(me - steps, row_devices)])
    rows = jnp.take(long_sources, partners, axis=0)
    hit = (rows // NB) == me
    earlier = jnp.arange(SLOTS)[None, :] < jnp.arange(SLOTS)[:, None]
    rank = jnp.sum((hit[:, None, :] & earlier[None]).astype(jnp.int32), axis=2)
    local = rows % NB
    picks = [jnp.sum(jnp.where(hit & (rank == q), local, 0), axis=1) for q in range(2)]
    table = jnp.stack(picks, 1)
    return table[: len(shifts())], table[len(shifts()):]


def own_slot_pairs(long_sources, me, row_devices):
    source = lax.dynamic_index_in_dim(long_sources, me, 0, keepdims=False)
    owner = source // NB
    offset = jnp.mod(owner - me, row_devices)
    offset = jnp.where(offset > row_devices // 2, offset - row_devices, offset)
    same = (owner[:, None] == owner[None, :]) & (
        jnp.arange(SLOTS)[None, :] < jnp.arange(SLOTS)[:, None]
    )
    rank = jnp.sum(same.astype(jnp.int32), axis=1)
    send_position = jnp.where(offset < 0, offset + REACH, offset + REACH - 1)
    read_position = jnp.where(offset > 0, -offset + REACH, -offset + REACH - 1)
    return send_position * 2 + rank, read_position * 2 + rank


def inverse_of(pairs):
    return jnp.sum(
        jnp.where(pairs[None, :] == jnp.arange(SLOTS)[:, None], jnp.arange(SLOTS)[None, :], 0), axis=1
    )


def forward_sum(blocks, prev_edge, next_edge, panels, band_blocks, long_in_order, targets_in_order):
    earlier = jnp.concatenate([prev_edge[:, None], blocks[:, :-1]], 1)
    onward = jnp.concatenate([blocks[:, 1:], next_edge[:, None]], 1)
    near = jnp.einsum("fbm,bnm->fbn", earlier, band_blocks[:, 0], preferred_element_type=jnp.float32)
    near = near + jnp.einsum("fbm,bnm->fbn", blocks, band_blocks[:, 1], preferred_element_type=jnp.float32)
    near = near + jnp.einsum("fbm,bnm->fbn", onward, band_blocks[:, 2], preferred_element_type=jnp.float32)
    contrib = jnp.einsum("kfm,knm->kfn", panels, long_in_order, preferred_element_type=jnp.float32)
    far = jnp.einsum("kb,kfn->fbn", targets_in_order, contrib, precision=HI)
    return near + far


def local(
    features,
    weight_in,
    weight_out,
    score_grad,
    band_blocks,
    long_blocks,
    long_rows,
    long_sources,
    long_counts,
):
    row_devices = lax.axis_size("row")
    col_devices = lax.axis_size("col")
    me = lax.axis_index("row")
    col_index = lax.axis_index("col")
    row_ids = long_rows[0]
    hidden_count = weight_in.shape[1]
    class_count = score_grad.shape[0]
    nodes = features.shape[1]
    h_rows = hidden_count
    f_rows = features.shape[0]
    c_rows = class_count
    hf_rows = h_rows + f_rows
    up = shift_index(1)
    down = shift_index(-1)

    live_count = lax.dynamic_index_in_dim(long_counts, me, 0, keepdims=False)
    is_live = jnp.arange(SLOTS, dtype=jnp.int32) < live_count
    live = is_live.astype(jnp.float32)
    targets = (
        (row_ids[:, None] == jnp.arange(NB, dtype=jnp.int32)[None, :]) & is_live[:, None]
    ).astype(jnp.float32)
    send_pair, read_pair = own_slot_pairs(long_sources, me, row_devices)
    sending_slot = inverse_of(send_pair)
    reading_slot = inverse_of(read_pair)
    long_read = jnp.take(long_blocks, reading_slot, axis=0)
    targets_read = jnp.take(targets, reading_slot, axis=0)
    wanted, landing_blocks = slot_tables(long_sources, me, row_devices)
    edge_block = jnp.array([[NB - 1 if e == 1 else 0] for e in shifts()], jnp.int32)
    pick = jnp.concatenate([wanted, edge_block], 1).reshape(-1)

    hidden_in = jnp.einsum(
        "ih,in->hn", weight_in, features, preferred_element_type=jnp.float32
    ).astype(jnp.bfloat16)
    both_in = jnp.concatenate([hidden_in, features], 0)
    both_blocks = both_in.reshape(hf_rows, NB, BLK)

    sg_blocks = score_grad.reshape(class_count, NB, BLK)
    sg_prior = jnp.einsum("fbn,bnm->fbm", sg_blocks, band_blocks[:, 0], preferred_element_type=jnp.float32)
    sg_middle = jnp.einsum("fbn,bnm->fbm", sg_blocks, band_blocks[:, 1], preferred_element_type=jnp.float32)
    sg_later = jnp.einsum("fbn,bnm->fbm", sg_blocks, band_blocks[:, 2], preferred_element_type=jnp.float32)
    sg_rows = jnp.take(sg_blocks, jnp.take(row_ids, sending_slot), axis=1)
    sg_out = jnp.einsum(
        "fkn,knm->kfm", sg_rows, jnp.take(long_blocks, sending_slot, axis=0),
        preferred_element_type=jnp.float32,
    )
    sg_out = sg_out * jnp.take(live, sending_slot)[:, None, None]
    sg_edges = jnp.zeros((len(shifts()), 1, c_rows, BLK), jnp.float32)
    sg_edges = sg_edges.at[up, 0].set(sg_later[:, NB - 1]).at[down, 0].set(sg_prior[:, 0])
    sg_send = jnp.concatenate([sg_out.reshape(len(shifts()), 2, c_rows, BLK), sg_edges], 1)

    picked = jnp.take(both_blocks.transpose(1, 0, 2), pick, axis=0)
    picked = picked.reshape(len(shifts()), 3, hf_rows, BLK).astype(jnp.float32)
    send_all = jnp.concatenate([picked, sg_send], 2)
    arrived = [send_by(send_all[i], "row", e) for i, e in enumerate(shifts())]
    pairs_in = jnp.concatenate([a[:2] for a in arrived], 0)

    both_sum = forward_sum(
        both_blocks,
        arrived[up][2, :hf_rows].astype(jnp.bfloat16),
        arrived[down][2, :hf_rows].astype(jnp.bfloat16),
        pairs_in[:, :hf_rows].astype(jnp.bfloat16),
        band_blocks,
        long_read,
        targets_read,
    )
    hidden_sum = both_sum[:h_rows].reshape(h_rows, nodes)
    feat_sum = both_sum[h_rows:].reshape(f_rows, nodes)

    landing = (
        landing_blocks.reshape(-1)[:, None] == jnp.arange(NB, dtype=jnp.int32)[None, :]
    ).astype(jnp.float32)
    sg_sum = (
        sg_middle
        + jnp.concatenate([sg_prior[:, 1:], arrived[down][2, hf_rows:][:, None]], 1)
        + jnp.concatenate([arrived[up][2, hf_rows:][:, None], sg_later[:, :-1]], 1)
        + jnp.einsum("kb,kfm->fbm", landing, pairs_in[:, hf_rows:], precision=HI)
    )
    class_back = sg_sum.reshape(c_rows, nodes).astype(jnp.bfloat16)

    hidden_act = jax.nn.silu(hidden_sum).astype(jnp.bfloat16)

    my_rows = lax.dynamic_slice_in_dim(weight_out, col_index * hidden_count, hidden_count, 0)
    class_part = jnp.einsum("hc,hn->cn", my_rows, hidden_act, preferred_element_type=jnp.float32)
    part_blocks = class_part.reshape(col_devices, c_rows, nodes)
    mine = jnp.broadcast_to(class_back.astype(jnp.float32)[None], part_blocks.shape)
    outgoing = jnp.stack([part_blocks, mine], 1)
    incoming = lax.all_to_all(outgoing, "col", 0, 0, tiled=True)
    class_in = jnp.sum(incoming[:, 0], axis=0).astype(jnp.bfloat16)
    all_back = incoming[:, 1].astype(jnp.bfloat16).reshape(col_devices * c_rows, nodes)

    hidden_back = jnp.einsum("hc,cn->hn", my_rows, all_back, preferred_element_type=jnp.float32)
    second_part = jnp.einsum("hn,cn->hc", hidden_act, all_back, preferred_element_type=jnp.float32)

    sigmoid_val = jax.nn.sigmoid(hidden_sum)
    slope_back = (hidden_back * sigmoid_val * (1.0 + hidden_sum * (1.0 - sigmoid_val))).astype(
        jnp.bfloat16
    )
    first_part = jnp.einsum(
        "in,hn->ih", feat_sum, slope_back.astype(jnp.float32), precision=HI
    )

    flat = jnp.concatenate([first_part.reshape(-1), second_part.reshape(-1)])
    pieces = lax.all_to_all(flat.reshape(row_devices, -1), "row", 0, 0, tiled=True)
    class_blocks = class_in.reshape(c_rows, NB, BLK)
    class_pick = jnp.take(class_blocks.transpose(1, 0, 2), pick, axis=0)
    class_pick = class_pick.reshape(len(shifts()), 3, c_rows, BLK)
    lanes = jnp.zeros((row_devices,) + class_pick.shape[1:], class_pick.dtype)
    for i, e in enumerate(shifts()):
        lanes = lanes.at[e % row_devices].set(class_pick[i])
    doubled = jnp.concatenate([lanes, lanes], 0)
    lanes = lax.dynamic_slice_in_dim(doubled, jnp.mod(row_devices - me, row_devices), row_devices, 0)

    flat = jnp.concatenate([first_part.reshape(-1), second_part.reshape(-1)])
    width = flat.size // row_devices
    outgoing = jnp.concatenate(
        [flat.reshape(row_devices, width), lanes.astype(jnp.float32).reshape(row_devices, -1)], 1
    )
    incoming = lax.all_to_all(outgoing, "row", 0, 0, tiled=True)
    pieces = incoming[:, :width]
    from_rows = incoming[:, width:].reshape((row_devices,) + class_pick.shape[1:])
    doubled = jnp.concatenate([from_rows, from_rows], 0)
    near = lax.dynamic_slice_in_dim(doubled, jnp.mod(me - REACH, row_devices), 2 * REACH + 1, 0)
    class_arrived = [near[REACH - e].astype(jnp.bfloat16) for e in shifts()]
    class_pairs = jnp.concatenate([x[:2] for x in class_arrived], 0)
    scores = forward_sum(
        class_blocks,
        class_arrived[up][2],
        class_arrived[down][2],
        class_pairs,
        band_blocks,
        long_read,
        targets_read,
    ).reshape(c_rows, nodes).astype(jnp.bfloat16)

    summed = jnp.sum(pieces, axis=0, keepdims=True)
    spread = jnp.broadcast_to(summed, (row_devices, summed.shape[1]))
    flat = lax.all_to_all(spread, "row", 0, 0, tiled=True).reshape(-1)
    first_grad = flat[: first_part.size].reshape(first_part.shape)
    second_grad = flat[first_part.size:].reshape(second_part.shape)
    return (scores, first_grad, second_grad)


def solution(mesh):
    return jax.shard_map(
        local,
        mesh=mesh,
        in_specs=(
            P(None, "row"),
            P(None, "col"),
            P(),
            P("col", "row"),
            P("row", None, None, None),
            P("row", None, None),
            P("row", None),
            P(),
            P(),
        ),
        out_specs=(P("col", "row"), P(None, "col"), P("col", None)),
        check_vma=False,
    )
```

```python
import jax
import jax.numpy as jnp
from jax import lax
from jax.sharding import PartitionSpec as P

BLK = 128
NB = 16
REACH = 3
SLOTS = 12
HI = lax.Precision.HIGHEST


def shifts():
    return [e for e in range(-REACH, REACH + 1) if e != 0]


def shift_index(e):
    return e + REACH if e < 0 else e + REACH - 1


def send_by(x, axis, by):
    devices = lax.axis_size(axis)
    return lax.ppermute(x, axis, [(i, (i + by) % devices) for i in range(devices)])


def swap_with(x, axis, mask):
    devices = lax.axis_size(axis)
    return lax.ppermute(x, axis, [(i, i ^ mask) for i in range(devices)])


def slot_tables(long_sources, me, row_devices):
    steps = jnp.array(shifts(), jnp.int32)
    partners = jnp.concatenate([jnp.mod(me + steps, row_devices), jnp.mod(me - steps, row_devices)])
    rows = jnp.take(long_sources, partners, axis=0)
    hit = (rows // NB) == me
    earlier = jnp.arange(SLOTS)[None, :] < jnp.arange(SLOTS)[:, None]
    rank = jnp.sum((hit[:, None, :] & earlier[None]).astype(jnp.int32), axis=2)
    local = rows % NB
    picks = [jnp.sum(jnp.where(hit & (rank == q), local, 0), axis=1) for q in range(2)]
    table = jnp.stack(picks, 1)
    return table[: len(shifts())], table[len(shifts()):]


def own_slot_pairs(long_sources, me, row_devices):
    source = lax.dynamic_index_in_dim(long_sources, me, 0, keepdims=False)
    owner = source // NB
    offset = jnp.mod(owner - me, row_devices)
    offset = jnp.where(offset > row_devices // 2, offset - row_devices, offset)
    same = (owner[:, None] == owner[None, :]) & (
        jnp.arange(SLOTS)[None, :] < jnp.arange(SLOTS)[:, None]
    )
    rank = jnp.sum(same.astype(jnp.int32), axis=1)
    send_position = jnp.where(offset < 0, offset + REACH, offset + REACH - 1)
    read_position = jnp.where(offset > 0, -offset + REACH, -offset + REACH - 1)
    return send_position * 2 + rank, read_position * 2 + rank


def inverse_of(pairs):
    return jnp.sum(
        jnp.where(pairs[None, :] == jnp.arange(SLOTS)[:, None], jnp.arange(SLOTS)[None, :], 0), axis=1
    )


def forward_sum(blocks, prev_edge, next_edge, panels, band_blocks, long_in_order, targets_in_order):
    earlier = jnp.concatenate([prev_edge[:, None], blocks[:, :-1]], 1)
    onward = jnp.concatenate([blocks[:, 1:], next_edge[:, None]], 1)
    near = jnp.einsum("fbm,bnm->fbn", earlier, band_blocks[:, 0], preferred_element_type=jnp.float32)
    near = near + jnp.einsum("fbm,bnm->fbn", blocks, band_blocks[:, 1], preferred_element_type=jnp.float32)
    near = near + jnp.einsum("fbm,bnm->fbn", onward, band_blocks[:, 2], preferred_element_type=jnp.float32)
    contrib = jnp.einsum("kfm,knm->kfn", panels, long_in_order, preferred_element_type=jnp.float32)
    far = jnp.einsum("kb,kfn->fbn", targets_in_order, contrib, precision=HI)
    return near + far


def local(
    features,
    weight_in,
    weight_out,
    score_grad,
    band_blocks,
    long_blocks,
    long_rows,
    long_sources,
    long_counts,
):
    row_devices = lax.axis_size("row")
    col_devices = lax.axis_size("col")
    me = lax.axis_index("row")
    col_index = lax.axis_index("col")
    row_ids = long_rows[0]
    hidden_count = weight_in.shape[1]
    class_count = score_grad.shape[0]
    nodes = features.shape[1]
    h_rows = hidden_count
    f_rows = features.shape[0]
    c_rows = class_count
    hf_rows = h_rows + f_rows
    up = shift_index(1)
    down = shift_index(-1)

    live_count = lax.dynamic_index_in_dim(long_counts, me, 0, keepdims=False)
    is_live = jnp.arange(SLOTS, dtype=jnp.int32) < live_count
    live = is_live.astype(jnp.float32)
    targets = (
        (row_ids[:, None] == jnp.arange(NB, dtype=jnp.int32)[None, :]) & is_live[:, None]
    ).astype(jnp.float32)
    send_pair, read_pair = own_slot_pairs(long_sources, me, row_devices)
    sending_slot = inverse_of(send_pair)
    reading_slot = inverse_of(read_pair)
    long_read = jnp.take(long_blocks, reading_slot, axis=0)
    targets_read = jnp.take(targets, reading_slot, axis=0)
    wanted, landing_blocks = slot_tables(long_sources, me, row_devices)
    edge_block = jnp.array([[NB - 1 if e == 1 else 0] for e in shifts()], jnp.int32)
    pick = jnp.concatenate([wanted, edge_block], 1).reshape(-1)

    hidden_in = jnp.einsum(
        "ih,in->hn", weight_in, features, preferred_element_type=jnp.float32
    ).astype(jnp.bfloat16)
    both_in = jnp.concatenate([hidden_in, features], 0)
    both_blocks = both_in.reshape(hf_rows, NB, BLK)

    sg_blocks = score_grad.reshape(class_count, NB, BLK)
    sg_prior = jnp.einsum("fbn,bnm->fbm", sg_blocks, band_blocks[:, 0], preferred_element_type=jnp.float32)
    sg_middle = jnp.einsum("fbn,bnm->fbm", sg_blocks, band_blocks[:, 1], preferred_element_type=jnp.float32)
    sg_later = jnp.einsum("fbn,bnm->fbm", sg_blocks, band_blocks[:, 2], preferred_element_type=jnp.float32)
    sg_rows = jnp.take(sg_blocks, jnp.take(row_ids, sending_slot), axis=1)
    sg_out = jnp.einsum(
        "fkn,knm->kfm", sg_rows, jnp.take(long_blocks, sending_slot, axis=0),
        preferred_element_type=jnp.float32,
    )
    sg_out = sg_out * jnp.take(live, sending_slot)[:, None, None]
    sg_edges = jnp.zeros((len(shifts()), 1, c_rows, BLK), jnp.float32)
    sg_edges = sg_edges.at[up, 0].set(sg_later[:, NB - 1]).at[down, 0].set(sg_prior[:, 0])
    sg_send = jnp.concatenate([sg_out.reshape(len(shifts()), 2, c_rows, BLK), sg_edges], 1)

    picked = jnp.take(both_blocks.transpose(1, 0, 2), pick, axis=0)
    picked = picked.reshape(len(shifts()), 3, hf_rows, BLK).astype(jnp.float32)
    send_all = jnp.concatenate([picked, sg_send], 2)
    arrived = [send_by(send_all[i], "row", e) for i, e in enumerate(shifts())]
    pairs_in = jnp.concatenate([a[:2] for a in arrived], 0)

    both_sum = forward_sum(
        both_blocks,
        arrived[up][2, :hf_rows].astype(jnp.bfloat16),
        arrived[down][2, :hf_rows].astype(jnp.bfloat16),
        pairs_in[:, :hf_rows].astype(jnp.bfloat16),
        band_blocks,
        long_read,
        targets_read,
    )
    hidden_sum = both_sum[:h_rows].reshape(h_rows, nodes)
    feat_sum = both_sum[h_rows:].reshape(f_rows, nodes)

    landing = (
        landing_blocks.reshape(-1)[:, None] == jnp.arange(NB, dtype=jnp.int32)[None, :]
    ).astype(jnp.float32)
    sg_sum = (
        sg_middle
        + jnp.concatenate([sg_prior[:, 1:], arrived[down][2, hf_rows:][:, None]], 1)
        + jnp.concatenate([arrived[up][2, hf_rows:][:, None], sg_later[:, :-1]], 1)
        + jnp.einsum("kb,kfm->fbm", landing, pairs_in[:, hf_rows:], precision=HI)
    )
    class_back = sg_sum.reshape(c_rows, nodes).astype(jnp.bfloat16)

    hidden_act = jax.nn.silu(hidden_sum).astype(jnp.bfloat16)

    my_rows = lax.dynamic_slice_in_dim(weight_out, col_index * hidden_count, hidden_count, 0)
    class_part = jnp.einsum("hc,hn->cn", my_rows, hidden_act, preferred_element_type=jnp.float32)
    part_blocks = class_part.reshape(col_devices, c_rows, nodes)
    lead = lax.reduce_precision(part_blocks, exponent_bits=8, mantissa_bits=7)
    rest = (part_blocks - lead).astype(jnp.bfloat16)
    mine = jnp.broadcast_to(class_back[None], part_blocks.shape)
    outgoing = jnp.stack([lead.astype(jnp.bfloat16), rest, mine], 1)
    incoming = lax.all_to_all(outgoing, "col", 0, 0, tiled=True)
    class_in = jnp.sum(
        incoming[:, 0].astype(jnp.float32) + incoming[:, 1].astype(jnp.float32), axis=0
    ).astype(jnp.bfloat16)
    all_back = incoming[:, 2].reshape(col_devices * c_rows, nodes)

    hidden_back = jnp.einsum("hc,cn->hn", my_rows, all_back, preferred_element_type=jnp.float32)
    second_part = jnp.einsum("hn,cn->hc", hidden_act, all_back, preferred_element_type=jnp.float32)

    sigmoid_val = jax.nn.sigmoid(hidden_sum)
    slope_back = (hidden_back * sigmoid_val * (1.0 + hidden_sum * (1.0 - sigmoid_val))).astype(
        jnp.bfloat16
    )
    first_part = jnp.einsum(
        "in,hn->ih", feat_sum, slope_back.astype(jnp.float32), precision=HI
    )

    flat = jnp.concatenate([first_part.reshape(-1), second_part.reshape(-1)])
    pieces = lax.all_to_all(flat.reshape(row_devices, -1), "row", 0, 0, tiled=True)
    class_blocks = class_in.reshape(c_rows, NB, BLK)
    class_pick = jnp.take(class_blocks.transpose(1, 0, 2), pick, axis=0)
    class_pick = class_pick.reshape(len(shifts()), 3, c_rows, BLK)
    class_pick, pieces = lax.optimization_barrier((class_pick, pieces))
    class_arrived = [send_by(class_pick[i], "row", e) for i, e in enumerate(shifts())]
    class_pairs = jnp.concatenate([a[:2] for a in class_arrived], 0)
    scores = forward_sum(
        class_blocks,
        class_arrived[up][2],
        class_arrived[down][2],
        class_pairs,
        band_blocks,
        long_read,
        targets_read,
    ).reshape(c_rows, nodes).astype(jnp.bfloat16)

    summed = jnp.sum(pieces, axis=0, keepdims=True)
    spread = jnp.broadcast_to(summed, (row_devices, summed.shape[1]))
    flat = lax.all_to_all(spread, "row", 0, 0, tiled=True).reshape(-1)
    first_grad = flat[: first_part.size].reshape(first_part.shape)
    second_grad = flat[first_part.size:].reshape(second_part.shape)
    return (scores, first_grad, second_grad)


def solution(mesh):
    return jax.shard_map(
        local,
        mesh=mesh,
        in_specs=(
            P(None, "row"),
            P(None, "col"),
            P(),
            P("col", "row"),
            P("row", None, None, None),
            P("row", None, None),
            P("row", None),
            P(),
            P(),
        ),
        out_specs=(P("col", "row"), P(None, "col"), P("col", None)),
        check_vma=False,
    )
```

```python
import jax
import jax.numpy as jnp
from jax import lax
from jax.sharding import PartitionSpec as P

BLK = 128
NB = 16
REACH = 3
SLOTS = 12
HI = lax.Precision.HIGHEST


def shifts():
    return [e for e in range(-REACH, REACH + 1) if e != 0]


def shift_index(e):
    return e + REACH if e < 0 else e + REACH - 1


def send_by(x, axis, by):
    devices = lax.axis_size(axis)
    return lax.ppermute(x, axis, [(i, (i + by) % devices) for i in range(devices)])


def swap_with(x, axis, mask):
    devices = lax.axis_size(axis)
    return lax.ppermute(x, axis, [(i, i ^ mask) for i in range(devices)])


def slot_tables(long_sources, me, row_devices):
    steps = jnp.array(shifts(), jnp.int32)
    partners = jnp.concatenate([jnp.mod(me + steps, row_devices), jnp.mod(me - steps, row_devices)])
    rows = jnp.take(long_sources, partners, axis=0)
    hit = (rows // NB) == me
    earlier = jnp.arange(SLOTS)[None, :] < jnp.arange(SLOTS)[:, None]
    rank = jnp.sum((hit[:, None, :] & earlier[None]).astype(jnp.int32), axis=2)
    local = rows % NB
    picks = [jnp.sum(jnp.where(hit & (rank == q), local, 0), axis=1) for q in range(2)]
    table = jnp.stack(picks, 1)
    return table[: len(shifts())], table[len(shifts()):]


def own_slot_pairs(long_sources, me, row_devices):
    source = lax.dynamic_index_in_dim(long_sources, me, 0, keepdims=False)
    owner = source // NB
    offset = jnp.mod(owner - me, row_devices)
    offset = jnp.where(offset > row_devices // 2, offset - row_devices, offset)
    same = (owner[:, None] == owner[None, :]) & (
        jnp.arange(SLOTS)[None, :] < jnp.arange(SLOTS)[:, None]
    )
    rank = jnp.sum(same.astype(jnp.int32), axis=1)
    send_position = jnp.where(offset < 0, offset + REACH, offset + REACH - 1)
    read_position = jnp.where(offset > 0, -offset + REACH, -offset + REACH - 1)
    return send_position * 2 + rank, read_position * 2 + rank


def inverse_of(pairs):
    return jnp.sum(
        jnp.where(pairs[None, :] == jnp.arange(SLOTS)[:, None], jnp.arange(SLOTS)[None, :], 0), axis=1
    )


def forward_sum(blocks, prev_edge, next_edge, panels, band_blocks, long_in_order, targets_in_order):
    earlier = jnp.concatenate([prev_edge[:, None], blocks[:, :-1]], 1)
    onward = jnp.concatenate([blocks[:, 1:], next_edge[:, None]], 1)
    near = jnp.einsum("fbm,bnm->fbn", earlier, band_blocks[:, 0], preferred_element_type=jnp.float32)
    near = near + jnp.einsum("fbm,bnm->fbn", blocks, band_blocks[:, 1], preferred_element_type=jnp.float32)
    near = near + jnp.einsum("fbm,bnm->fbn", onward, band_blocks[:, 2], preferred_element_type=jnp.float32)
    contrib = jnp.einsum("kfm,knm->kfn", panels, long_in_order, preferred_element_type=jnp.float32)
    far = jnp.einsum("kb,kfn->fbn", targets_in_order, contrib, precision=HI)
    return near + far


def local(
    features,
    weight_in,
    weight_out,
    score_grad,
    band_blocks,
    long_blocks,
    long_rows,
    long_sources,
    long_counts,
):
    row_devices = lax.axis_size("row")
    col_devices = lax.axis_size("col")
    me = lax.axis_index("row")
    col_index = lax.axis_index("col")
    row_ids = long_rows[0]
    hidden_count = weight_in.shape[1]
    class_count = score_grad.shape[0]
    nodes = features.shape[1]
    h_rows = hidden_count
    f_rows = features.shape[0]
    c_rows = class_count
    hf_rows = h_rows + f_rows
    up = shift_index(1)
    down = shift_index(-1)

    live_count = lax.dynamic_index_in_dim(long_counts, me, 0, keepdims=False)
    is_live = jnp.arange(SLOTS, dtype=jnp.int32) < live_count
    live = is_live.astype(jnp.float32)
    targets = (
        (row_ids[:, None] == jnp.arange(NB, dtype=jnp.int32)[None, :]) & is_live[:, None]
    ).astype(jnp.float32)
    send_pair, read_pair = own_slot_pairs(long_sources, me, row_devices)
    sending_slot = inverse_of(send_pair)
    reading_slot = inverse_of(read_pair)
    long_read = jnp.take(long_blocks, reading_slot, axis=0)
    targets_read = jnp.take(targets, reading_slot, axis=0)
    wanted, landing_blocks = slot_tables(long_sources, me, row_devices)
    edge_block = jnp.array([[NB - 1 if e == 1 else 0] for e in shifts()], jnp.int32)
    pick = jnp.concatenate([wanted, edge_block], 1).reshape(-1)

    hidden_in = jnp.einsum(
        "ih,in->hn", weight_in, features, preferred_element_type=jnp.float32
    ).astype(jnp.bfloat16)
    both_in = jnp.concatenate([hidden_in, features], 0)
    both_blocks = both_in.reshape(hf_rows, NB, BLK)

    sg_blocks = score_grad.reshape(class_count, NB, BLK)
    sg_prior = jnp.einsum("fbn,bnm->fbm", sg_blocks, band_blocks[:, 0], preferred_element_type=jnp.float32)
    sg_middle = jnp.einsum("fbn,bnm->fbm", sg_blocks, band_blocks[:, 1], preferred_element_type=jnp.float32)
    sg_later = jnp.einsum("fbn,bnm->fbm", sg_blocks, band_blocks[:, 2], preferred_element_type=jnp.float32)
    sg_rows = jnp.take(sg_blocks, jnp.take(row_ids, sending_slot), axis=1)
    sg_out = jnp.einsum(
        "fkn,knm->kfm", sg_rows, jnp.take(long_blocks, sending_slot, axis=0),
        preferred_element_type=jnp.float32,
    )
    sg_out = sg_out * jnp.take(live, sending_slot)[:, None, None]
    sg_edges = jnp.zeros((len(shifts()), 1, c_rows, BLK), jnp.float32)
    sg_edges = sg_edges.at[up, 0].set(sg_later[:, NB - 1]).at[down, 0].set(sg_prior[:, 0])
    sg_send = jnp.concatenate([sg_out.reshape(len(shifts()), 2, c_rows, BLK), sg_edges], 1)

    picked = jnp.take(both_blocks.transpose(1, 0, 2), pick, axis=0)
    picked = picked.reshape(len(shifts()), 3, hf_rows, BLK).astype(jnp.float32)
    send_all = jnp.concatenate([picked, sg_send], 2)
    arrived = [send_by(send_all[i], "row", e) for i, e in enumerate(shifts())]
    pairs_in = jnp.concatenate([a[:2] for a in arrived], 0)

    both_sum = forward_sum(
        both_blocks,
        arrived[up][2, :hf_rows].astype(jnp.bfloat16),
        arrived[down][2, :hf_rows].astype(jnp.bfloat16),
        pairs_in[:, :hf_rows].astype(jnp.bfloat16),
        band_blocks,
        long_read,
        targets_read,
    )
    hidden_sum = both_sum[:h_rows].reshape(h_rows, nodes)
    feat_sum = both_sum[h_rows:].reshape(f_rows, nodes)

    landing = (
        landing_blocks.reshape(-1)[:, None] == jnp.arange(NB, dtype=jnp.int32)[None, :]
    ).astype(jnp.float32)
    sg_sum = (
        sg_middle
        + jnp.concatenate([sg_prior[:, 1:], arrived[down][2, hf_rows:][:, None]], 1)
        + jnp.concatenate([arrived[up][2, hf_rows:][:, None], sg_later[:, :-1]], 1)
        + jnp.einsum("kb,kfm->fbm", landing, pairs_in[:, hf_rows:], precision=HI)
    )
    class_back = sg_sum.reshape(c_rows, nodes).astype(jnp.bfloat16)

    hidden_act = jax.nn.silu(hidden_sum).astype(jnp.bfloat16)

    my_rows = lax.dynamic_slice_in_dim(weight_out, col_index * hidden_count, hidden_count, 0)
    class_part = jnp.einsum("hc,hn->cn", my_rows, hidden_act, preferred_element_type=jnp.float32)
    part_blocks = class_part.reshape(col_devices, c_rows, nodes)
    mine = jnp.broadcast_to(class_back[None], part_blocks.shape)
    outgoing = jnp.stack([part_blocks.astype(jnp.bfloat16), mine], 1)
    incoming = lax.all_to_all(outgoing, "col", 0, 0, tiled=True)
    class_in = jnp.sum(incoming[:, 0].astype(jnp.float32), axis=0).astype(jnp.bfloat16)
    all_back = incoming[:, 1].reshape(col_devices * c_rows, nodes)

    hidden_back = jnp.einsum("hc,cn->hn", my_rows, all_back, preferred_element_type=jnp.float32)
    second_part = jnp.einsum("hn,cn->hc", hidden_act, all_back, preferred_element_type=jnp.float32)

    sigmoid_val = jax.nn.sigmoid(hidden_sum)
    slope_back = (hidden_back * sigmoid_val * (1.0 + hidden_sum * (1.0 - sigmoid_val))).astype(
        jnp.bfloat16
    )
    first_part = jnp.einsum(
        "in,hn->ih", feat_sum, slope_back.astype(jnp.float32), precision=HI
    )

    flat = jnp.concatenate([first_part.reshape(-1), second_part.reshape(-1)])
    pieces = lax.all_to_all(flat.reshape(row_devices, -1), "row", 0, 0, tiled=True)
    class_blocks = class_in.reshape(c_rows, NB, BLK)
    class_pick = jnp.take(class_blocks.transpose(1, 0, 2), pick, axis=0)
    class_pick = class_pick.reshape(len(shifts()), 3, c_rows, BLK)
    class_pick, pieces = lax.optimization_barrier((class_pick, pieces))
    class_arrived = [send_by(class_pick[i], "row", e) for i, e in enumerate(shifts())]
    class_pairs = jnp.concatenate([a[:2] for a in class_arrived], 0)
    scores = forward_sum(
        class_blocks,
        class_arrived[up][2],
        class_arrived[down][2],
        class_pairs,
        band_blocks,
        long_read,
        targets_read,
    ).reshape(c_rows, nodes).astype(jnp.bfloat16)

    summed = jnp.sum(pieces, axis=0, keepdims=True)
    spread = jnp.broadcast_to(summed, (row_devices, summed.shape[1]))
    flat = lax.all_to_all(spread, "row", 0, 0, tiled=True).reshape(-1)
    first_grad = flat[: first_part.size].reshape(first_part.shape)
    second_grad = flat[first_part.size:].reshape(second_part.shape)
    return (scores, first_grad, second_grad)


def solution(mesh):
    return jax.shard_map(
        local,
        mesh=mesh,
        in_specs=(
            P(None, "row"),
            P(None, "col"),
            P(),
            P("col", "row"),
            P("row", None, None, None),
            P("row", None, None),
            P("row", None),
            P(),
            P(),
        ),
        out_specs=(P("col", "row"), P(None, "col"), P("col", None)),
        check_vma=False,
    )
```

```python
import jax
import jax.numpy as jnp
from jax import lax
from jax.sharding import PartitionSpec as P

BLK = 128
NB = 16
REACH = 3
SLOTS = 12
HI = lax.Precision.HIGHEST


def shifts():
    return [e for e in range(-REACH, REACH + 1) if e != 0]


def shift_index(e):
    return e + REACH if e < 0 else e + REACH - 1


def send_by(x, axis, by):
    devices = lax.axis_size(axis)
    return lax.ppermute(x, axis, [(i, (i + by) % devices) for i in range(devices)])


def swap_with(x, axis, mask):
    devices = lax.axis_size(axis)
    return lax.ppermute(x, axis, [(i, i ^ mask) for i in range(devices)])


def slot_tables(long_sources, me, row_devices):
    steps = jnp.array(shifts(), jnp.int32)
    partners = jnp.concatenate([jnp.mod(me + steps, row_devices), jnp.mod(me - steps, row_devices)])
    rows = jnp.take(long_sources, partners, axis=0)
    hit = (rows // NB) == me
    earlier = jnp.arange(SLOTS)[None, :] < jnp.arange(SLOTS)[:, None]
    rank = jnp.sum((hit[:, None, :] & earlier[None]).astype(jnp.int32), axis=2)
    local = rows % NB
    picks = [jnp.sum(jnp.where(hit & (rank == q), local, 0), axis=1) for q in range(2)]
    table = jnp.stack(picks, 1)
    return table[: len(shifts())], table[len(shifts()):]


def own_slot_pairs(long_sources, me, row_devices):
    source = lax.dynamic_index_in_dim(long_sources, me, 0, keepdims=False)
    owner = source // NB
    offset = jnp.mod(owner - me, row_devices)
    offset = jnp.where(offset > row_devices // 2, offset - row_devices, offset)
    same = (owner[:, None] == owner[None, :]) & (
        jnp.arange(SLOTS)[None, :] < jnp.arange(SLOTS)[:, None]
    )
    rank = jnp.sum(same.astype(jnp.int32), axis=1)
    send_position = jnp.where(offset < 0, offset + REACH, offset + REACH - 1)
    read_position = jnp.where(offset > 0, -offset + REACH, -offset + REACH - 1)
    return send_position * 2 + rank, read_position * 2 + rank


def inverse_of(pairs):
    return jnp.sum(
        jnp.where(pairs[None, :] == jnp.arange(SLOTS)[:, None], jnp.arange(SLOTS)[None, :], 0), axis=1
    )


def forward_sum(blocks, prev_edge, next_edge, panels, band_blocks, long_in_order, targets_in_order):
    earlier = jnp.concatenate([prev_edge[:, None], blocks[:, :-1]], 1)
    onward = jnp.concatenate([blocks[:, 1:], next_edge[:, None]], 1)
    near = jnp.einsum("fbm,bnm->fbn", earlier, band_blocks[:, 0], preferred_element_type=jnp.float32)
    near = near + jnp.einsum("fbm,bnm->fbn", blocks, band_blocks[:, 1], preferred_element_type=jnp.float32)
    near = near + jnp.einsum("fbm,bnm->fbn", onward, band_blocks[:, 2], preferred_element_type=jnp.float32)
    contrib = jnp.einsum("kfm,knm->kfn", panels, long_in_order, preferred_element_type=jnp.float32)
    far = jnp.einsum("kb,kfn->fbn", targets_in_order, contrib, precision=HI)
    return near + far


def local(
    features,
    weight_in,
    weight_out,
    score_grad,
    band_blocks,
    long_blocks,
    long_rows,
    long_sources,
    long_counts,
):
    row_devices = lax.axis_size("row")
    col_devices = lax.axis_size("col")
    me = lax.axis_index("row")
    col_index = lax.axis_index("col")
    row_ids = long_rows[0]
    hidden_count = weight_in.shape[1]
    class_count = score_grad.shape[0]
    nodes = features.shape[1]
    h_rows = hidden_count
    f_rows = features.shape[0]
    c_rows = class_count
    hf_rows = h_rows + f_rows
    up = shift_index(1)
    down = shift_index(-1)

    live_count = lax.dynamic_index_in_dim(long_counts, me, 0, keepdims=False)
    is_live = jnp.arange(SLOTS, dtype=jnp.int32) < live_count
    live = is_live.astype(jnp.float32)
    targets = (
        (row_ids[:, None] == jnp.arange(NB, dtype=jnp.int32)[None, :]) & is_live[:, None]
    ).astype(jnp.float32)
    send_pair, read_pair = own_slot_pairs(long_sources, me, row_devices)
    sending_slot = inverse_of(send_pair)
    reading_slot = inverse_of(read_pair)
    long_read = jnp.take(long_blocks, reading_slot, axis=0)
    targets_read = jnp.take(targets, reading_slot, axis=0)
    wanted, landing_blocks = slot_tables(long_sources, me, row_devices)
    edge_block = jnp.array([[NB - 1 if e == 1 else 0] for e in shifts()], jnp.int32)
    pick = jnp.concatenate([wanted, edge_block], 1).reshape(-1)

    hidden_in = jnp.einsum(
        "ih,in->hn", weight_in, features, preferred_element_type=jnp.float32
    ).astype(jnp.bfloat16)
    both_in = jnp.concatenate([hidden_in, features], 0)
    both_blocks = both_in.reshape(hf_rows, NB, BLK)

    sg_blocks = score_grad.reshape(class_count, NB, BLK)
    sg_prior = jnp.einsum("fbn,bnm->fbm", sg_blocks, band_blocks[:, 0], preferred_element_type=jnp.float32)
    sg_middle = jnp.einsum("fbn,bnm->fbm", sg_blocks, band_blocks[:, 1], preferred_element_type=jnp.float32)
    sg_later = jnp.einsum("fbn,bnm->fbm", sg_blocks, band_blocks[:, 2], preferred_element_type=jnp.float32)
    sg_rows = jnp.take(sg_blocks, jnp.take(row_ids, sending_slot), axis=1)
    sg_out = jnp.einsum(
        "fkn,knm->kfm", sg_rows, jnp.take(long_blocks, sending_slot, axis=0),
        preferred_element_type=jnp.float32,
    )
    sg_out = sg_out * jnp.take(live, sending_slot)[:, None, None]
    sg_edges = jnp.zeros((len(shifts()), 1, c_rows, BLK), jnp.float32)
    sg_edges = sg_edges.at[up, 0].set(sg_later[:, NB - 1]).at[down, 0].set(sg_prior[:, 0])
    sg_send = jnp.concatenate([sg_out.reshape(len(shifts()), 2, c_rows, BLK), sg_edges], 1)

    picked = jnp.take(both_blocks.transpose(1, 0, 2), pick, axis=0)
    picked = picked.reshape(len(shifts()), 3, hf_rows, BLK).astype(jnp.float32)
    send_all = jnp.concatenate([picked, sg_send], 2)
    arrived = [send_by(send_all[i], "row", e) for i, e in enumerate(shifts())]
    pairs_in = jnp.concatenate([a[:2] for a in arrived], 0)

    both_sum = forward_sum(
        both_blocks,
        arrived[up][2, :hf_rows].astype(jnp.bfloat16),
        arrived[down][2, :hf_rows].astype(jnp.bfloat16),
        pairs_in[:, :hf_rows].astype(jnp.bfloat16),
        band_blocks,
        long_read,
        targets_read,
    )
    hidden_sum = both_sum[:h_rows].reshape(h_rows, nodes)
    feat_sum = both_sum[h_rows:].reshape(f_rows, nodes)

    landing = (
        landing_blocks.reshape(-1)[:, None] == jnp.arange(NB, dtype=jnp.int32)[None, :]
    ).astype(jnp.float32)
    sg_sum = (
        sg_middle
        + jnp.concatenate([sg_prior[:, 1:], arrived[down][2, hf_rows:][:, None]], 1)
        + jnp.concatenate([arrived[up][2, hf_rows:][:, None], sg_later[:, :-1]], 1)
        + jnp.einsum("kb,kfm->fbm", landing, pairs_in[:, hf_rows:], precision=HI)
    )
    class_back = sg_sum.reshape(c_rows, nodes).astype(jnp.bfloat16)

    hidden_act = jax.nn.silu(hidden_sum).astype(jnp.bfloat16)

    my_rows = lax.dynamic_slice_in_dim(weight_out, col_index * hidden_count, hidden_count, 0)
    class_part = jnp.einsum("hc,hn->cn", my_rows, hidden_act, preferred_element_type=jnp.float32)
    part_blocks = class_part.reshape(col_devices, c_rows, nodes)
    lead = lax.reduce_precision(part_blocks, exponent_bits=8, mantissa_bits=7)
    rest = (part_blocks - lead).astype(jnp.bfloat16)
    mine = jnp.broadcast_to(class_back[None], part_blocks.shape)
    outgoing = jnp.stack([lead.astype(jnp.bfloat16), rest, mine], 1)
    incoming = lax.all_to_all(outgoing, "col", 0, 0, tiled=True)
    class_in = jnp.sum(
        incoming[:, 0].astype(jnp.float32) + incoming[:, 1].astype(jnp.float32), axis=0
    ).astype(jnp.bfloat16)
    all_back = incoming[:, 2].reshape(col_devices * c_rows, nodes)

    hidden_back = jnp.einsum("hc,cn->hn", my_rows, all_back, preferred_element_type=jnp.float32)
    second_part = jnp.einsum("hn,cn->hc", hidden_act, all_back, preferred_element_type=jnp.float32)

    sigmoid_val = jax.nn.sigmoid(hidden_sum)
    slope_back = (hidden_back * sigmoid_val * (1.0 + hidden_sum * (1.0 - sigmoid_val))).astype(
        jnp.bfloat16
    )
    first_part = jnp.einsum(
        "in,hn->ih", feat_sum, slope_back.astype(jnp.float32), precision=HI
    )

    flat = jnp.concatenate([first_part.reshape(-1), second_part.reshape(-1)])
    flat = flat + swap_with(flat, "row", 1)
    halves = flat.reshape(row_devices, 2, -1)
    own_half = lax.dynamic_index_in_dim(halves, me % 2, 1, keepdims=False)
    arrived_halves = lax.all_to_all(own_half, "row", 0, 0, tiled=True)
    pieces = arrived_halves.reshape(row_devices // 2, -1)
    class_blocks = class_in.reshape(c_rows, NB, BLK)
    class_pick = jnp.take(class_blocks.transpose(1, 0, 2), pick, axis=0)
    class_pick = class_pick.reshape(len(shifts()), 3, c_rows, BLK)
    class_pick, pieces = lax.optimization_barrier((class_pick, pieces))
    class_arrived = [send_by(class_pick[i], "row", e) for i, e in enumerate(shifts())]
    class_pairs = jnp.concatenate([a[:2] for a in class_arrived], 0)
    scores = forward_sum(
        class_blocks,
        class_arrived[up][2],
        class_arrived[down][2],
        class_pairs,
        band_blocks,
        long_read,
        targets_read,
    ).reshape(c_rows, nodes).astype(jnp.bfloat16)

    summed = jnp.sum(pieces, axis=0, keepdims=True)
    spread = jnp.broadcast_to(summed, (row_devices, summed.shape[1]))
    flat = lax.all_to_all(spread, "row", 0, 0, tiled=True).reshape(-1)
    first_grad = flat[: first_part.size].reshape(first_part.shape)
    second_grad = flat[first_part.size:].reshape(second_part.shape)
    return (scores, first_grad, second_grad)


def solution(mesh):
    return jax.shard_map(
        local,
        mesh=mesh,
        in_specs=(
            P(None, "row"),
            P(None, "col"),
            P(),
            P("col", "row"),
            P("row", None, None, None),
            P("row", None, None),
            P("row", None),
            P(),
            P(),
        ),
        out_specs=(P("col", "row"), P(None, "col"), P("col", None)),
        check_vma=False,
    )
```

```python
import jax
import jax.numpy as jnp
from jax import lax
from jax.sharding import PartitionSpec as P

BLK = 128
NB = 16
REACH = 3
SLOTS = 12
HI = lax.Precision.HIGHEST


def shifts():
    return [e for e in range(-REACH, REACH + 1) if e != 0]


def shift_index(e):
    return e + REACH if e < 0 else e + REACH - 1


def send_by(x, axis, by):
    devices = lax.axis_size(axis)
    return lax.ppermute(x, axis, [(i, (i + by) % devices) for i in range(devices)])


def swap_with(x, axis, mask):
    devices = lax.axis_size(axis)
    return lax.ppermute(x, axis, [(i, i ^ mask) for i in range(devices)])


def slot_tables(long_sources, me, row_devices):
    steps = jnp.array(shifts(), jnp.int32)
    partners = jnp.concatenate([jnp.mod(me + steps, row_devices), jnp.mod(me - steps, row_devices)])
    rows = jnp.take(long_sources, partners, axis=0)
    hit = (rows // NB) == me
    earlier = jnp.arange(SLOTS)[None, :] < jnp.arange(SLOTS)[:, None]
    rank = jnp.sum((hit[:, None, :] & earlier[None]).astype(jnp.int32), axis=2)
    local = rows % NB
    picks = [jnp.sum(jnp.where(hit & (rank == q), local, 0), axis=1) for q in range(2)]
    table = jnp.stack(picks, 1)
    return table[: len(shifts())], table[len(shifts()):]


def own_slot_pairs(long_sources, me, row_devices):
    source = lax.dynamic_index_in_dim(long_sources, me, 0, keepdims=False)
    owner = source // NB
    offset = jnp.mod(owner - me, row_devices)
    offset = jnp.where(offset > row_devices // 2, offset - row_devices, offset)
    same = (owner[:, None] == owner[None, :]) & (
        jnp.arange(SLOTS)[None, :] < jnp.arange(SLOTS)[:, None]
    )
    rank = jnp.sum(same.astype(jnp.int32), axis=1)
    send_position = jnp.where(offset < 0, offset + REACH, offset + REACH - 1)
    read_position = jnp.where(offset > 0, -offset + REACH, -offset + REACH - 1)
    return send_position * 2 + rank, read_position * 2 + rank


def inverse_of(pairs):
    return jnp.sum(
        jnp.where(pairs[None, :] == jnp.arange(SLOTS)[:, None], jnp.arange(SLOTS)[None, :], 0), axis=1
    )


def forward_sum(blocks, prev_edge, next_edge, panels, band_blocks, long_in_order, targets_in_order):
    earlier = jnp.concatenate([prev_edge[:, None], blocks[:, :-1]], 1)
    onward = jnp.concatenate([blocks[:, 1:], next_edge[:, None]], 1)
    near = jnp.einsum("fbm,bnm->fbn", earlier, band_blocks[:, 0], preferred_element_type=jnp.float32)
    near = near + jnp.einsum("fbm,bnm->fbn", blocks, band_blocks[:, 1], preferred_element_type=jnp.float32)
    near = near + jnp.einsum("fbm,bnm->fbn", onward, band_blocks[:, 2], preferred_element_type=jnp.float32)
    contrib = jnp.einsum("kfm,knm->kfn", panels, long_in_order, preferred_element_type=jnp.float32)
    far = jnp.einsum("kb,kfn->fbn", targets_in_order, contrib, precision=HI)
    return near + far


def local(
    features,
    weight_in,
    weight_out,
    score_grad,
    band_blocks,
    long_blocks,
    long_rows,
    long_sources,
    long_counts,
):
    row_devices = lax.axis_size("row")
    col_devices = lax.axis_size("col")
    me = lax.axis_index("row")
    col_index = lax.axis_index("col")
    row_ids = long_rows[0]
    hidden_count = weight_in.shape[1]
    class_count = score_grad.shape[0]
    nodes = features.shape[1]
    h_rows = hidden_count
    f_rows = features.shape[0]
    c_rows = class_count
    hf_rows = h_rows + f_rows
    up = shift_index(1)
    down = shift_index(-1)

    live_count = lax.dynamic_index_in_dim(long_counts, me, 0, keepdims=False)
    is_live = jnp.arange(SLOTS, dtype=jnp.int32) < live_count
    live = is_live.astype(jnp.float32)
    targets = (
        (row_ids[:, None] == jnp.arange(NB, dtype=jnp.int32)[None, :]) & is_live[:, None]
    ).astype(jnp.float32)
    send_pair, read_pair = own_slot_pairs(long_sources, me, row_devices)
    sending_slot = inverse_of(send_pair)
    reading_slot = inverse_of(read_pair)
    long_read = jnp.take(long_blocks, reading_slot, axis=0)
    targets_read = jnp.take(targets, reading_slot, axis=0)
    wanted, landing_blocks = slot_tables(long_sources, me, row_devices)
    edge_block = jnp.array([[NB - 1 if e == 1 else 0] for e in shifts()], jnp.int32)
    pick = jnp.concatenate([wanted, edge_block], 1).reshape(-1)

    hidden_in = jnp.einsum(
        "ih,in->hn", weight_in, features, preferred_element_type=jnp.float32
    ).astype(jnp.bfloat16)
    both_in = jnp.concatenate([hidden_in, features], 0)
    both_blocks = both_in.reshape(hf_rows, NB, BLK)

    sg_blocks = score_grad.reshape(class_count, NB, BLK)
    sg_prior = jnp.einsum("fbn,bnm->fbm", sg_blocks, band_blocks[:, 0], preferred_element_type=jnp.float32)
    sg_middle = jnp.einsum("fbn,bnm->fbm", sg_blocks, band_blocks[:, 1], preferred_element_type=jnp.float32)
    sg_later = jnp.einsum("fbn,bnm->fbm", sg_blocks, band_blocks[:, 2], preferred_element_type=jnp.float32)
    sg_rows = jnp.take(sg_blocks, jnp.take(row_ids, sending_slot), axis=1)
    sg_out = jnp.einsum(
        "fkn,knm->kfm", sg_rows, jnp.take(long_blocks, sending_slot, axis=0),
        preferred_element_type=jnp.float32,
    )
    sg_out = sg_out * jnp.take(live, sending_slot)[:, None, None]
    sg_edges = jnp.zeros((len(shifts()), 1, c_rows, BLK), jnp.float32)
    sg_edges = sg_edges.at[up, 0].set(sg_later[:, NB - 1]).at[down, 0].set(sg_prior[:, 0])
    sg_send = jnp.concatenate([sg_out.reshape(len(shifts()), 2, c_rows, BLK), sg_edges], 1)

    picked = jnp.take(both_blocks.transpose(1, 0, 2), pick, axis=0)
    picked = picked.reshape(len(shifts()), 3, hf_rows, BLK).astype(jnp.float32)
    send_all = jnp.concatenate([picked, sg_send], 2)
    arrived = [
        send_by(send_all[i] if abs(e) == 1 else send_all[i, :2], "row", e)
        for i, e in enumerate(shifts())
    ]
    pairs_in = jnp.concatenate([a[:2] for a in arrived], 0)

    both_sum = forward_sum(
        both_blocks,
        arrived[up][2, :hf_rows].astype(jnp.bfloat16),
        arrived[down][2, :hf_rows].astype(jnp.bfloat16),
        pairs_in[:, :hf_rows].astype(jnp.bfloat16),
        band_blocks,
        long_read,
        targets_read,
    )
    hidden_sum = both_sum[:h_rows].reshape(h_rows, nodes)
    feat_sum = both_sum[h_rows:].reshape(f_rows, nodes)

    landing = (
        landing_blocks.reshape(-1)[:, None] == jnp.arange(NB, dtype=jnp.int32)[None, :]
    ).astype(jnp.float32)
    sg_sum = (
        sg_middle
        + jnp.concatenate([sg_prior[:, 1:], arrived[down][2, hf_rows:][:, None]], 1)
        + jnp.concatenate([arrived[up][2, hf_rows:][:, None], sg_later[:, :-1]], 1)
        + jnp.einsum("kb,kfm->fbm", landing, pairs_in[:, hf_rows:], precision=HI)
    )
    class_back = sg_sum.reshape(c_rows, nodes).astype(jnp.bfloat16)

    hidden_act = jax.nn.silu(hidden_sum).astype(jnp.bfloat16)

    my_rows = lax.dynamic_slice_in_dim(weight_out, col_index * hidden_count, hidden_count, 0)
    class_part = jnp.einsum("hc,hn->cn", my_rows, hidden_act, preferred_element_type=jnp.float32)
    part_blocks = class_part.reshape(col_devices, c_rows, nodes)
    lead = lax.reduce_precision(part_blocks, exponent_bits=8, mantissa_bits=7)
    rest = (part_blocks - lead).astype(jnp.bfloat16)
    mine = jnp.broadcast_to(class_back[None], part_blocks.shape)
    outgoing = jnp.stack([lead.astype(jnp.bfloat16), rest, mine], 1)
    incoming = lax.all_to_all(outgoing, "col", 0, 0, tiled=True)
    class_in = jnp.sum(
        incoming[:, 0].astype(jnp.float32) + incoming[:, 1].astype(jnp.float32), axis=0
    ).astype(jnp.bfloat16)
    all_back = incoming[:, 2].reshape(col_devices * c_rows, nodes)

    hidden_back = jnp.einsum("hc,cn->hn", my_rows, all_back, preferred_element_type=jnp.float32)
    second_part = jnp.einsum("hn,cn->hc", hidden_act, all_back, preferred_element_type=jnp.float32)

    sigmoid_val = jax.nn.sigmoid(hidden_sum)
    slope_back = (hidden_back * sigmoid_val * (1.0 + hidden_sum * (1.0 - sigmoid_val))).astype(
        jnp.bfloat16
    )
    first_part = jnp.einsum(
        "in,hn->ih", feat_sum, slope_back.astype(jnp.float32), precision=HI
    )

    flat = jnp.concatenate([first_part.reshape(-1), second_part.reshape(-1)])
    pieces = lax.all_to_all(flat.reshape(row_devices, -1), "row", 0, 0, tiled=True)
    class_blocks = class_in.reshape(c_rows, NB, BLK)
    class_pick = jnp.take(class_blocks.transpose(1, 0, 2), pick, axis=0)
    class_pick = class_pick.reshape(len(shifts()), 3, c_rows, BLK)
    class_pick, pieces = lax.optimization_barrier((class_pick, pieces))
    class_arrived = [send_by(class_pick[i], "row", e) for i, e in enumerate(shifts())]
    class_pairs = jnp.concatenate([a[:2] for a in class_arrived], 0)
    scores = forward_sum(
        class_blocks,
        class_arrived[up][2],
        class_arrived[down][2],
        class_pairs,
        band_blocks,
        long_read,
        targets_read,
    ).reshape(c_rows, nodes).astype(jnp.bfloat16)

    summed = jnp.sum(pieces, axis=0, keepdims=True)
    spread = jnp.broadcast_to(summed, (row_devices, summed.shape[1]))
    flat = lax.all_to_all(spread, "row", 0, 0, tiled=True).reshape(-1)
    first_grad = flat[: first_part.size].reshape(first_part.shape)
    second_grad = flat[first_part.size:].reshape(second_part.shape)
    return (scores, first_grad, second_grad)


def solution(mesh):
    return jax.shard_map(
        local,
        mesh=mesh,
        in_specs=(
            P(None, "row"),
            P(None, "col"),
            P(),
            P("col", "row"),
            P("row", None, None, None),
            P("row", None, None),
            P("row", None),
            P(),
            P(),
        ),
        out_specs=(P("col", "row"), P(None, "col"), P("col", None)),
        check_vma=False,
    )
```
